32 devices in a mesh: section: 4 (over z), ctx: 8 (over y, x, core).
Axes of the slice: x: 2, y: 2, z: 4, core: 2. Of those that a mesh axis runs over, the one named last changes fastest.
Arguments:
- inputs: bfloat16 [4, 1024, 2048], P('section', 'ctx'), may hold values from -6 to 6
- out_grad: bfloat16 [4, 1024, 2048], P('section', 'ctx'), may hold values from -6 to 6
- gains: float32 [4, 3, 2048], P('section'), may hold values from 0.25 to 1.75
- exponent: int32 [4, 16, 16], P('section', 'ctx'), may hold values from 1 to 2048, as said below
- boundary: int32 [4, 16], P('section', 'ctx'), may hold values 0 or 1
Outputs:
- passed: bfloat16 [4, 1024, 2048], P('section', 'ctx')
The draws below stay inside these ranges and needn't reach their ends.
Inputs may be any that keep to these rules, and one draw needn't show every extreme that they name: Every group's tokens of head h decay by 1 - exponent / 65536 a token; every exponent is a power of two or twice one.
All inputs are finite; a program needn't handle non-finite values. No bound on the sum of `boundary` on one device may be relied on, other than what follows from the above.
Results may differ from the reference program's by a relative error of at most 0.0053.
Values may be sent and summed in bfloat16 or wider, within the bound.
No kernel may reach another device: no remote copies, remote signals or barrier semaphores. Data moves between devices by JAX's collectives and lax.ppermute only.
A program may use at most 192 MiB of HBM per device.

```python
import math
import jax
import jax.numpy as jnp
from jax import lax

H = 16
TOK_DEV = 128
F = 2048
TOKENS = 1024
NC = 16
LAYERS = 4
N_CTX = 8


def draw_exponent(key, part):
    key_level, key_head, key_twice, key_spot = jax.random.split(key, 4)
    level = jax.random.randint(key_level, (LAYERS, H), 0, 11)
    chosen = jax.random.randint(key_head, (LAYERS, 1), 0, H)
    head_ids = jnp.arange(H)[None, :]
    level = jnp.where(head_ids == chosen, 10, level)
    level = jnp.where(head_ids == (chosen + 1) % H, 0, level)
    twice = jax.random.randint(key_twice, (LAYERS, NC, H), 0, 2)
    spot = jax.random.randint(key_spot, (LAYERS, 1, 1), 0, NC)
    group_ids = jnp.arange(NC)[None, :, None]
    head_three = jnp.arange(H)[None, None, :]
    chosen_three = chosen[:, :, None]
    twice = jnp.where((group_ids == spot) & (head_three == chosen_three), 1, twice)
    twice = jnp.where((group_ids == spot) & (head_three == (chosen_three + 1) % H), 0, twice)
    power = jnp.left_shift(jnp.ones_like(level), level)
    return (power[:, None, :] * (1 + twice)).astype(jnp.int32)


def plant(drawn, own_key, low, top_value):
    dims = drawn.shape
    spot = [jax.random.randint(jax.random.fold_in(own_key, axis), (), 0, dims[axis]) for axis in range(len(dims))]
    drawn = drawn.at[tuple(spot)].set(low)
    longest = dims.index(max(dims))
    spot[longest] = (spot[longest] + 1) % dims[longest]
    return drawn.at[tuple(spot)].set(top_value)


def level_of(rng, dims, shards, least, largest):
    loudness, own = 1.0, jax.random.fold_in(rng, 6)
    for position, shards_of in shards:
        draws = jnp.exp(jax.random.uniform(jax.random.fold_in(own, position), (shards_of,), jnp.float32, least / len(shards), largest / len(shards)))
        loudness = loudness * jnp.repeat(draws, dims[position] // shards_of).reshape([-1 if axis == position else 1 for axis in range(len(dims))])
    return loudness


def normal_values(key, dims, scale, limit, cuts=(), kind=jnp.bfloat16):
    values = jax.random.normal(key, dims, jnp.float32) * scale
    if len(cuts) > 0:
        values = level_of(key, dims, cuts, -0.22, 0.18) * values
    return jnp.clip(values, min=-limit, max=limit).astype(kind)


def setup_inputs(seed: int = 0) -> dict:
    keys = jax.random.split(jax.random.key(seed), 6)
    inputs = normal_values(keys[0], (LAYERS, TOKENS, F), 1.0, 6.0, ((0, 4), (1, 8)))
    out_grad = normal_values(keys[1], (LAYERS, TOKENS, F), 1.0, 6.0, ((0, 4), (1, 8)))
    gains = jnp.clip(1.0 + 0.15 * jax.random.normal(keys[2], (LAYERS, 3, F), jnp.float32), 0.25, 1.75)
    exponent = draw_exponent(jax.random.fold_in(keys[5], 71), 0)
    boundary = plant((jax.random.randint(keys[4], (LAYERS, NC), 0, 64) < 1).astype(jnp.int32), jax.random.fold_in(keys[4], 1), 0, 1)
    return {"inputs": inputs, "out_grad": out_grad, "gains": gains, "exponent": exponent, "boundary": boundary}


HIGH = lax.Precision.HIGHEST


def decay_logs(exponent, boundary, length):
    count, heads = exponent.shape
    rate = jnp.log(1.0 - exponent.astype(jnp.float32) / 65536.0)
    spread = jnp.broadcast_to(rate[:, None, :], (count, length, heads))
    opening = (jnp.arange(length) == 0)[None, :, None] & (boundary == 1)[:, None, None]
    return spread + jnp.where(opening, math.log(0.5), 0.0).astype(spread.dtype)


def projections(inputs, gain, heads):
    rows = inputs.shape[0]
    widened = inputs.astype(jnp.float32)
    result = []
    for index in range(3):
        rounded = lax.optimization_barrier((widened * gain[index]).astype(jnp.bfloat16))
        result.append(rounded.astype(jnp.float32).reshape(rows, heads, -1))
    return result


def local_decay(cumul, lower):
    cum_heads = cumul.T
    gap = cum_heads[:, :, None] - cum_heads[:, None, :]
    return jnp.where(lower[None], jnp.exp(jnp.minimum(gap, 0.0)), 0.0)


def contribution(inputs, out_grad, gain, exponent, boundary):
    rows, width = inputs.shape
    count, heads = exponent.shape
    head_dim = width // heads
    length = rows // count
    scale = 1.0 / head_dim
    queries, key_rows, value_rows = projections(inputs, gain, heads)
    grad_rows = out_grad.astype(jnp.float32).reshape(rows, heads, head_dim)
    logs = decay_logs(exponent, boundary, length)
    lower = jnp.arange(length)[:, None] >= jnp.arange(length)[None, :]

    def blocks(array):
        return array.reshape(count, length, heads, head_dim)

    items = (blocks(queries), blocks(key_rows), blocks(value_rows), blocks(grad_rows), logs)

    def forward(state, item):
        query_c, key_c, value_c, grad_c, log_c = item
        cumul = jnp.cumsum(log_c, axis=0)
        decay = local_decay(cumul, lower)
        mixing = jnp.einsum('thd,shd->hts', grad_c, value_c, precision=HIGH) * decay
        inner = jnp.einsum('hts,shd->thd', mixing, key_c, precision=HIGH)
        carried = jnp.exp(cumul)[:, :, None] * jnp.einsum('the,hde->thd', grad_c, state, precision=HIGH)
        tail = jnp.exp(cumul[-1][None, :] - cumul)
        update = jnp.einsum('shd,she->hde', key_c * tail[:, :, None], value_c, precision=HIGH)
        return jnp.exp(cumul[-1])[:, None, None] * state + update, scale * (inner + carried)

    def backward(adjoint, item):
        query_c, key_c, value_c, grad_c, log_c = item
        cumul = jnp.cumsum(log_c, axis=0)
        decay = local_decay(cumul, lower)
        mixing = jnp.einsum('thd,shd->hts', grad_c, value_c, precision=HIGH) * decay
        key_inner = jnp.einsum('hts,thd->shd', mixing, query_c, precision=HIGH)
        attention = jnp.einsum('thd,shd->hts', query_c, key_c, precision=HIGH) * decay
        value_inner = jnp.einsum('hts,the->she', attention, grad_c, precision=HIGH)
        tail = jnp.exp(cumul[-1][None, :] - cumul)[:, :, None]
        key_far = tail * jnp.einsum('she,hde->shd', value_c, adjoint, precision=HIGH)
        value_far = tail * jnp.einsum('shd,hde->she', key_c, adjoint, precision=HIGH)
        update = scale * jnp.einsum('shd,she->hde', query_c * jnp.exp(cumul)[:, :, None], grad_c, precision=HIGH)
        new_adjoint = jnp.exp(cumul[-1])[:, None, None] * adjoint + update
        return new_adjoint, (scale * key_inner + key_far, scale * value_inner + value_far)

    empty = jnp.zeros((heads, head_dim, head_dim), jnp.float32)
    final_state, query_grad = lax.scan(forward, empty, items)
    first_adjoint, pair = lax.scan(backward, empty, items, reverse=True)
    key_grad, value_grad = pair
    total = gain[0] * query_grad.reshape(rows, width)
    total = total + gain[1] * key_grad.reshape(rows, width)
    total = total + gain[2] * value_grad.reshape(rows, width)
    return total


def layer_backward(inputs, out_grad, gain, exponent, boundary):
    rows, width = inputs.shape
    count, heads = exponent.shape
    whole = contribution(inputs, out_grad, gain, exponent, boundary)
    per_block = count // N_CTX
    pieces = (inputs.reshape(N_CTX, TOK_DEV, width), out_grad.reshape(N_CTX, TOK_DEV, width),
              exponent.reshape(N_CTX, per_block, heads), boundary.reshape(N_CTX, per_block))
    near_terms = lax.map(lambda item: contribution(item[0], item[1], gain, item[2], item[3]), pieces)
    near_terms = near_terms.reshape(rows, width)
    near_total = out_grad.astype(jnp.float32) + near_terms
    far_total = whole - near_terms
    near_round = lax.optimization_barrier(near_total.astype(jnp.bfloat16))
    far_round = lax.optimization_barrier(far_total.astype(jnp.bfloat16))
    return (near_round.astype(jnp.float32) + far_round.astype(jnp.float32)).astype(jnp.bfloat16)


def reference(inputs, out_grad, gains, exponent, boundary):
    grads = lax.map(lambda item: layer_backward(*item), (inputs, out_grad, gains, exponent, boundary))
    return jnp.roll(grads, -1, axis=0)
```

```python
import math

import jax
import jax.numpy as jnp
from jax import lax
from jax.sharding import PartitionSpec as P

CH = 64


HIGH = lax.Precision.HIGHEST


def shifted(value, axis, steps):
    count = lax.axis_size(axis)
    if steps >= 0:
        pairs = [(source, source + steps) for source in range(count - steps)]
    else:
        pairs = [(source, source + steps) for source in range(-steps, count)]
    return lax.ppermute(value, axis, pairs)


def merge(farther, nearer):
    return (farther[0] * nearer[0], nearer[0][:, None, None] * farther[1] + nearer[1])


def scan_in(item, axis, direction):
    count = lax.axis_size(axis)
    if count == 1:
        return jnp.zeros_like(item[1])
    window = item
    covered = 1
    while 2 * covered < count:
        window = merge(shifted(window, axis, direction * covered), window)
        covered *= 2
    nearer = shifted(window, axis, direction)
    if 1 + covered >= count:
        return nearer[1]
    farther = shifted(window[1], axis, direction * (1 + covered))
    return nearer[0][:, None, None] * farther + nearer[1]


def passed_along(value, axis, steps):
    count = lax.axis_size(axis)
    pairs = [(source, (source + steps) % count) for source in range(count)]
    return lax.ppermute(value, axis, pairs)


def decay_logs(exponent, boundary, length):
    count, heads = exponent.shape
    rate = jnp.log(1.0 - exponent.astype(jnp.float32) / 65536.0)
    spread = jnp.broadcast_to(rate[:, None, :], (count, length, heads))
    opening = (jnp.arange(length) == 0)[None, :, None] & (boundary == 1)[:, None, None]
    return spread + jnp.where(opening, math.log(0.5), 0.0).astype(spread.dtype)


def projections(inputs, gain, heads):
    rows = inputs.shape[0]
    widened = inputs.astype(jnp.float32)
    result = []
    for index in range(3):
        rounded = lax.optimization_barrier((widened * gain[index]).astype(jnp.bfloat16))
        result.append(rounded.reshape(rows, heads, -1))
    return result


def local(inputs, out_grad, gains, exponent, boundary):
    block = inputs[0]
    grad_block = out_grad[0]
    gain = gains[0]
    rows, width = block.shape
    heads = exponent.shape[2]
    head_dim = width // heads
    scale = 1.0 / head_dim
    query_half, key_half, value_half = projections(block, gain, heads)
    grad_half = grad_block.reshape(rows, heads, head_dim)
    queries = query_half.astype(jnp.float32)
    key_rows = key_half.astype(jnp.float32)
    value_rows = value_half.astype(jnp.float32)
    grad_rows = grad_half.astype(jnp.float32)
    logs = decay_logs(exponent[0], boundary[0], CH).reshape(rows, heads)
    cumul = jnp.cumsum(logs, axis=0)
    whole_decay = jnp.exp(cumul[-1])
    growth = jnp.exp(cumul)
    tail = jnp.exp(cumul[-1][None, :] - cumul)
    forward_part = jnp.einsum(
        "shd,she->hde", key_rows * tail[:, :, None], value_rows, precision=HIGH
    )
    adjoint_part = scale * jnp.einsum(
        "shd,she->hde", queries * growth[:, :, None], grad_rows, precision=HIGH
    )
    state_in = scan_in((whole_decay, forward_part), "ctx", 1)
    adjoint_in = scan_in((whole_decay, adjoint_part), "ctx", -1)
    cum_heads = cumul.T
    gap = cum_heads[:, :, None] - cum_heads[:, None, :]
    lower = jnp.arange(rows)[:, None] >= jnp.arange(rows)[None, :]
    decay = jnp.where(lower[None], jnp.exp(jnp.minimum(gap, 0.0)), 0.0)
    mixing = (
        jnp.einsum("thd,shd->hts", grad_half, value_half, preferred_element_type=jnp.float32)
        * decay
    )
    query_near = scale * jnp.einsum("hts,shd->thd", mixing, key_rows, precision=HIGH)
    key_near = scale * jnp.einsum("hts,thd->shd", mixing, queries, precision=HIGH)
    attention = (
        jnp.einsum("thd,shd->hts", query_half, key_half, preferred_element_type=jnp.float32) * decay
    )
    value_near = scale * jnp.einsum("hts,the->she", attention, grad_rows, precision=HIGH)
    near_total = grad_block.astype(jnp.float32)
    near_total = near_total + gain[0] * query_near.reshape(rows, width)
    near_total = near_total + gain[1] * key_near.reshape(rows, width)
    near_total = near_total + gain[2] * value_near.reshape(rows, width)
    near_round = near_total.astype(jnp.bfloat16)
    near_received = passed_along(near_round, "section", -1)
    query_far = (
        scale * growth[:, :, None] * jnp.einsum("the,hde->thd", grad_rows, state_in, precision=HIGH)
    )
    key_far = tail[:, :, None] * jnp.einsum("she,hde->shd", value_rows, adjoint_in, precision=HIGH)
    value_far = tail[:, :, None] * jnp.einsum("shd,hde->she", key_rows, adjoint_in, precision=HIGH)
    far_total = gain[0] * query_far.reshape(rows, width)
    far_total = far_total + gain[1] * key_far.reshape(rows, width)
    far_total = far_total + gain[2] * value_far.reshape(rows, width)
    far_round = far_total.astype(jnp.bfloat16)
    far_received = passed_along(far_round, "section", -1)
    near_kept, far_kept = lax.optimization_barrier((near_received, far_received))
    received = (near_kept.astype(jnp.float32) + far_kept.astype(jnp.float32)).astype(jnp.bfloat16)
    return received[None]


def solution(mesh):
    in_specs = (
        P("section", "ctx", None),
        P("section", "ctx", None),
        P("section", None, None),
        P("section", "ctx", None),
        P("section", "ctx"),
    )
    out_specs = P("section", "ctx", None)
    return jax.shard_map(local, mesh=mesh, in_specs=in_specs, out_specs=out_specs, check_vma=False)
```

```python
import math

import jax
import jax.numpy as jnp
from jax import lax
from jax.sharding import PartitionSpec as P

CH = 64


HIGH = lax.Precision.HIGHEST


def ranked(value, axis, forward, moves):
    count = lax.axis_size(axis)
    if forward:
        pairs = list(moves)
    else:
        pairs = [(count - 1 - source, count - 1 - target) for source, target in moves]
    return lax.ppermute(value, axis, pairs)


def span_decay(logs, low, high):
    spots = jnp.arange(logs.shape[0])[:, None]
    inside = (spots > low) & (spots < high)
    return jnp.exp(jnp.sum(jnp.where(inside, logs, 0.0), axis=0))[:, None, None]


def scan_in(part, block_logs, axis, forward):
    count = lax.axis_size(axis)
    if count == 1:
        return jnp.zeros_like(part)
    assert count % 2 == 0
    here = lax.axis_index(axis)
    rank = here if forward else count - 1 - here
    ordered = block_logs if forward else block_logs[::-1]
    couples = count // 2
    group = rank // 2
    lower = ranked(part, axis, forward, [(2 * p, 2 * p + 1) for p in range(couples)])
    own = jnp.exp(lax.dynamic_index_in_dim(ordered, rank, keepdims=False))[:, None, None]
    window = own * lower + part
    group_logs = ordered.reshape(couples, 2, -1).sum(axis=1)
    if couples <= 4:
        incoming = jnp.zeros_like(part)
        for step in range(1, couples):
            moves = [(2 * p + 1, 2 * (p + step) + 1) for p in range(couples - step)]
            got = ranked(window, axis, forward, moves)
            incoming = incoming + span_decay(group_logs, group - step, group) * got
    else:
        covered = 1
        while 2 * covered < couples:
            moves = [(2 * p + 1, 2 * (p + covered) + 1) for p in range(couples - covered)]
            got = ranked(window, axis, forward, moves)
            window = span_decay(group_logs, group - covered, group + 1) * got + window
            covered *= 2
        moves = [(2 * p + 1, 2 * p + 3) for p in range(couples - 1)]
        incoming = ranked(window, axis, forward, moves)
        if 1 + covered < couples:
            moves = [(2 * p + 1, 2 * (p + 1 + covered) + 1) for p in range(couples - 1 - covered)]
            got = ranked(window, axis, forward, moves)
            incoming = incoming + span_decay(group_logs, group - covered - 1, group) * got
    down = ranked(incoming, axis, forward, [(2 * p + 1, 2 * p) for p in range(couples)])
    previous = jnp.exp(lax.dynamic_index_in_dim(ordered, jnp.maximum(rank - 1, 0), keepdims=False))
    odd_value = previous[:, None, None] * incoming + lower
    return jnp.where(rank % 2 == 0, down, odd_value)


def passed_along(value, axis, steps):
    count = lax.axis_size(axis)
    pairs = [(source, (source + steps) % count) for source in range(count)]
    return lax.ppermute(value, axis, pairs)


def decay_logs(exponent, boundary, length):
    count, heads = exponent.shape
    rate = jnp.log(1.0 - exponent.astype(jnp.float32) / 65536.0)
    spread = jnp.broadcast_to(rate[:, None, :], (count, length, heads))
    opening = (jnp.arange(length) == 0)[None, :, None] & (boundary == 1)[:, None, None]
    return spread + jnp.where(opening, math.log(0.5), 0.0).astype(spread.dtype)


def projections(inputs, gain, heads):
    rows = inputs.shape[0]
    widened = inputs.astype(jnp.float32)
    result = []
    for index in range(3):
        rounded = lax.optimization_barrier((widened * gain[index]).astype(jnp.bfloat16))
        result.append(rounded.reshape(rows, heads, -1))
    return result


def local(inputs, out_grad, gains, exponent, boundary):
    block = inputs[0]
    grad_block = out_grad[0]
    gain = gains[0]
    rows, width = block.shape
    heads = exponent.shape[2]
    head_dim = width // heads
    scale = 1.0 / head_dim
    query_half, key_half, value_half = projections(block, gain, heads)
    grad_half = grad_block.reshape(rows, heads, head_dim)
    queries = query_half.astype(jnp.float32)
    key_rows = key_half.astype(jnp.float32)
    value_rows = value_half.astype(jnp.float32)
    grad_rows = grad_half.astype(jnp.float32)
    logs = decay_logs(exponent[0], boundary[0], CH).reshape(rows, heads)
    cumul = jnp.cumsum(logs, axis=0)
    growth = jnp.exp(cumul)
    tail = jnp.exp(cumul[-1][None, :] - cumul)
    forward_part = jnp.einsum(
        "shd,she->hde", key_rows * tail[:, :, None], value_rows, precision=HIGH
    )
    adjoint_part = scale * jnp.einsum(
        "shd,she->hde", queries * growth[:, :, None], grad_rows, precision=HIGH
    )
    block_logs = lax.all_gather(cumul[-1], "ctx")
    state_in = scan_in(forward_part, block_logs, "ctx", True)
    adjoint_in = scan_in(adjoint_part, block_logs, "ctx", False)
    cum_heads = cumul.T
    gap = cum_heads[:, :, None] - cum_heads[:, None, :]
    lower = jnp.arange(rows)[:, None] >= jnp.arange(rows)[None, :]
    decay = jnp.where(lower[None], jnp.exp(jnp.minimum(gap, 0.0)), 0.0)
    mixing = (
        jnp.einsum("thd,shd->hts", grad_half, value_half, preferred_element_type=jnp.float32)
        * decay
    )
    query_near = scale * jnp.einsum("hts,shd->thd", mixing, key_rows, precision=HIGH)
    key_near = scale * jnp.einsum("hts,thd->shd", mixing, queries, precision=HIGH)
    attention = (
        jnp.einsum("thd,shd->hts", query_half, key_half, preferred_element_type=jnp.float32) * decay
    )
    value_near = scale * jnp.einsum("hts,the->she", attention, grad_rows, precision=HIGH)
    near_total = grad_block.astype(jnp.float32)
    near_total = near_total + gain[0] * query_near.reshape(rows, width)
    near_total = near_total + gain[1] * key_near.reshape(rows, width)
    near_total = near_total + gain[2] * value_near.reshape(rows, width)
    near_round = near_total.astype(jnp.bfloat16)
    near_received = passed_along(near_round, "section", -1)
    near_received, state_in, adjoint_in = lax.optimization_barrier(
        (near_received, state_in, adjoint_in)
    )
    query_far = (
        scale * growth[:, :, None] * jnp.einsum("the,hde->thd", grad_rows, state_in, precision=HIGH)
    )
    key_far = tail[:, :, None] * jnp.einsum("she,hde->shd", value_rows, adjoint_in, precision=HIGH)
    value_far = tail[:, :, None] * jnp.einsum("shd,hde->she", key_rows, adjoint_in, precision=HIGH)
    far_total = gain[0] * query_far.reshape(rows, width)
    far_total = far_total + gain[1] * key_far.reshape(rows, width)
    far_total = far_total + gain[2] * value_far.reshape(rows, width)
    far_round = far_total.astype(jnp.bfloat16)
    far_received = passed_along(far_round, "section", -1)
    received = (near_received.astype(jnp.float32) + far_received.astype(jnp.float32)).astype(
        jnp.bfloat16
    )
    return received[None]


def solution(mesh):
    in_specs = (
        P("section", "ctx", None),
        P("section", "ctx", None),
        P("section", None, None),
        P("section", "ctx", None),
        P("section", "ctx"),
    )
    out_specs = P("section", "ctx", None)
    return jax.shard_map(local, mesh=mesh, in_specs=in_specs, out_specs=out_specs, check_vma=False)
```

```python
import math

import jax
import jax.numpy as jnp
from jax import lax
from jax.sharding import PartitionSpec as P

CH = 64


HIGH = lax.Precision.HIGHEST


def ranked(value, axis, forward, moves):
    count = lax.axis_size(axis)
    if forward:
        pairs = list(moves)
    else:
        pairs = [(count - 1 - source, count - 1 - target) for source, target in moves]
    return lax.ppermute(value, axis, pairs)


def packed(state, rate):
    tile = jnp.broadcast_to(rate[:, None, None], (state.shape[0], 8, state.shape[2]))
    return jnp.concatenate([state, tile], axis=1)


def unpacked(message):
    width = message.shape[1] - 8
    return message[:, :width], message[:, width, 0]


def merged(farther, nearer):
    far_state, far_rate = unpacked(farther)
    near_state, near_rate = unpacked(nearer)
    return packed(near_rate[:, None, None] * far_state + near_state, far_rate * near_rate)


def scan_in(part, rate, axis, forward):
    count = lax.axis_size(axis)
    if count == 1:
        return jnp.zeros_like(part)
    assert count % 2 == 0
    here = lax.axis_index(axis)
    rank = here if forward else count - 1 - here
    couples = count // 2
    moves = [(2 * p, 2 * p + 1) for p in range(couples)]
    lower, lower_rate = unpacked(ranked(packed(part, rate), axis, forward, moves))
    window = packed(rate[:, None, None] * lower + part, rate * lower_rate)
    if couples <= 4:
        incoming = jnp.zeros_like(part)
        weight = jnp.ones_like(rate)
        for step in range(1, couples):
            moves = [(2 * p + 1, 2 * (p + step) + 1) for p in range(couples - step)]
            got, got_rate = unpacked(ranked(window, axis, forward, moves))
            incoming = incoming + weight[:, None, None] * got
            weight = weight * got_rate
    else:
        covered = 1
        while 2 * covered < couples:
            moves = [(2 * p + 1, 2 * (p + covered) + 1) for p in range(couples - covered)]
            window = merged(ranked(window, axis, forward, moves), window)
            covered *= 2
        moves = [(2 * p + 1, 2 * p + 3) for p in range(couples - 1)]
        nearer = ranked(window, axis, forward, moves)
        if 1 + covered < couples:
            moves = [(2 * p + 1, 2 * (p + 1 + covered) + 1) for p in range(couples - 1 - covered)]
            nearer = merged(ranked(window, axis, forward, moves), nearer)
        incoming = unpacked(nearer)[0]
    down = ranked(incoming, axis, forward, [(2 * p + 1, 2 * p) for p in range(couples)])
    odd_value = lower_rate[:, None, None] * incoming + lower
    return jnp.where(rank % 2 == 0, down, odd_value)


def passed_along(value, axis, steps):
    count = lax.axis_size(axis)
    pairs = [(source, (source + steps) % count) for source in range(count)]
    return lax.ppermute(value, axis, pairs)


def decay_logs(exponent, boundary, length):
    count, heads = exponent.shape
    rate = jnp.log(1.0 - exponent.astype(jnp.float32) / 65536.0)
    spread = jnp.broadcast_to(rate[:, None, :], (count, length, heads))
    opening = (jnp.arange(length) == 0)[None, :, None] & (boundary == 1)[:, None, None]
    return spread + jnp.where(opening, math.log(0.5), 0.0).astype(spread.dtype)


def projections(inputs, gain, heads):
    rows = inputs.shape[0]
    widened = inputs.astype(jnp.float32)
    result = []
    for index in range(3):
        rounded = lax.optimization_barrier((widened * gain[index]).astype(jnp.bfloat16))
        result.append(rounded.reshape(rows, heads, -1))
    return result


def local(inputs, out_grad, gains, exponent, boundary):
    block = inputs[0]
    grad_block = out_grad[0]
    gain = gains[0]
    rows, width = block.shape
    heads = exponent.shape[2]
    head_dim = width // heads
    scale = 1.0 / head_dim
    query_half, key_half, value_half = projections(block, gain, heads)
    grad_half = grad_block.reshape(rows, heads, head_dim)
    queries = query_half.astype(jnp.float32)
    key_rows = key_half.astype(jnp.float32)
    value_rows = value_half.astype(jnp.float32)
    grad_rows = grad_half.astype(jnp.float32)
    logs = decay_logs(exponent[0], boundary[0], CH).reshape(rows, heads)
    cumul = jnp.cumsum(logs, axis=0)
    growth = jnp.exp(cumul)
    tail = jnp.exp(cumul[-1][None, :] - cumul)
    forward_part = jnp.einsum(
        "shd,she->hde", key_rows * tail[:, :, None], value_rows, precision=HIGH
    )
    adjoint_part = scale * jnp.einsum(
        "shd,she->hde", queries * growth[:, :, None], grad_rows, precision=HIGH
    )
    whole_decay = jnp.exp(cumul[-1])
    state_in = scan_in(forward_part, whole_decay, "ctx", True)
    adjoint_in = scan_in(adjoint_part, whole_decay, "ctx", False)
    cum_heads = cumul.T
    gap = cum_heads[:, :, None] - cum_heads[:, None, :]
    lower = jnp.arange(rows)[:, None] >= jnp.arange(rows)[None, :]
    decay = jnp.where(lower[None], jnp.exp(jnp.minimum(gap, 0.0)), 0.0)
    mixing = (
        jnp.einsum("thd,shd->hts", grad_half, value_half, preferred_element_type=jnp.float32)
        * decay
    )
    query_near = scale * jnp.einsum("hts,shd->thd", mixing, key_rows, precision=HIGH)
    key_near = scale * jnp.einsum("hts,thd->shd", mixing, queries, precision=HIGH)
    attention = (
        jnp.einsum("thd,shd->hts", query_half, key_half, preferred_element_type=jnp.float32) * decay
    )
    value_near = scale * jnp.einsum("hts,the->she", attention, grad_rows, precision=HIGH)
    near_total = grad_block.astype(jnp.float32)
    near_total = near_total + gain[0] * query_near.reshape(rows, width)
    near_total = near_total + gain[1] * key_near.reshape(rows, width)
    near_total = near_total + gain[2] * value_near.reshape(rows, width)
    near_round = near_total.astype(jnp.bfloat16)
    near_received = passed_along(near_round, "section", -1)
    near_received, state_in, adjoint_in = lax.optimization_barrier(
        (near_received, state_in, adjoint_in)
    )
    query_far = (
        scale * growth[:, :, None] * jnp.einsum("the,hde->thd", grad_rows, state_in, precision=HIGH)
    )
    key_far = tail[:, :, None] * jnp.einsum("she,hde->shd", value_rows, adjoint_in, precision=HIGH)
    value_far = tail[:, :, None] * jnp.einsum("shd,hde->she", key_rows, adjoint_in, precision=HIGH)
    far_total = gain[0] * query_far.reshape(rows, width)
    far_total = far_total + gain[1] * key_far.reshape(rows, width)
    far_total = far_total + gain[2] * value_far.reshape(rows, width)
    far_round = far_total.astype(jnp.bfloat16)
    far_received = passed_along(far_round, "section", -1)
    received = (near_received.astype(jnp.float32) + far_received.astype(jnp.float32)).astype(
        jnp.bfloat16
    )
    return received[None]


def solution(mesh):
    in_specs = (
        P("section", "ctx", None),
        P("section", "ctx", None),
        P("section", None, None),
        P("section", "ctx", None),
        P("section", "ctx"),
    )
    out_specs = P("section", "ctx", None)
    return jax.shard_map(local, mesh=mesh, in_specs=in_specs, out_specs=out_specs, check_vma=False)
```

```python
import math

import jax
import jax.numpy as jnp
from jax import lax
from jax.sharding import PartitionSpec as P

CH = 64


HIGH = lax.Precision.HIGHEST


def packed(state, rate):
    tile = jnp.broadcast_to(rate[:, None, None], (state.shape[0], 8, state.shape[2]))
    return jnp.concatenate([state, tile], axis=1)


def unpacked(message):
    width = message.shape[1] - 8
    return message[:, :width], message[:, width, 0]


def merged(farther, nearer):
    far_state, far_rate = unpacked(farther)
    near_state, near_rate = unpacked(nearer)
    return packed(near_rate[:, None, None] * far_state + near_state, far_rate * near_rate)


def both_ways(count, moves):
    return list(moves) + [(count - 1 - source, count - 1 - target) for source, target in moves]


def scans_in(forward_part, backward_part, rate, axis, held):
    count = lax.axis_size(axis)
    if count == 1:
        return jnp.zeros_like(forward_part), jnp.zeros_like(backward_part), held
    assert count % 2 == 0
    odd = lax.axis_index(axis) % 2 == 1
    couples = count // 2
    swap = [(2 * p, 2 * p + 1) for p in range(couples)] + [(2 * p + 1, 2 * p) for p in range(couples)]
    mine = jnp.where(odd, forward_part, backward_part)
    sent = packed(jnp.where(odd, backward_part, forward_part), rate)
    lower, lower_rate = unpacked(lax.ppermute(sent, axis, swap))
    window = packed(rate[:, None, None] * lower + mine, rate * lower_rate)
    if couples <= 4:
        incoming = jnp.zeros_like(mine)
        weight = jnp.ones_like(rate)
        for step in range(1, couples):
            moves = [(2 * p + 1, 2 * (p + step) + 1) for p in range(couples - step)]
            got, got_rate = unpacked(lax.ppermute(window, axis, both_ways(count, moves)))
            incoming = incoming + weight[:, None, None] * got
            weight = weight * got_rate
    else:
        covered = 1
        while 2 * covered < couples:
            moves = [(2 * p + 1, 2 * (p + covered) + 1) for p in range(couples - covered)]
            window = merged(lax.ppermute(window, axis, both_ways(count, moves)), window)
            covered *= 2
        moves = [(2 * p + 1, 2 * p + 3) for p in range(couples - 1)]
        nearer = lax.ppermute(window, axis, both_ways(count, moves))
        if 1 + covered < couples:
            moves = [(2 * p + 1, 2 * (p + 1 + covered) + 1) for p in range(couples - 1 - covered)]
            nearer = merged(lax.ppermute(window, axis, both_ways(count, moves)), nearer)
        incoming = unpacked(nearer)[0]
    incoming, held = lax.optimization_barrier((incoming, held))
    other = lax.ppermute(incoming, axis, swap)
    own = lower_rate[:, None, None] * incoming + lower
    return jnp.where(odd, own, other), jnp.where(odd, other, own), held


def passed_along(value, axis, steps):
    count = lax.axis_size(axis)
    pairs = [(source, (source + steps) % count) for source in range(count)]
    return lax.ppermute(value, axis, pairs)


def decay_logs(exponent, boundary, length):
    count, heads = exponent.shape
    rate = jnp.log(1.0 - exponent.astype(jnp.float32) / 65536.0)
    spread = jnp.broadcast_to(rate[:, None, :], (count, length, heads))
    opening = (jnp.arange(length) == 0)[None, :, None] & (boundary == 1)[:, None, None]
    return spread + jnp.where(opening, math.log(0.5), 0.0).astype(spread.dtype)


def projections(inputs, gain, heads):
    rows = inputs.shape[0]
    widened = inputs.astype(jnp.float32)
    result = []
    for index in range(3):
        rounded = lax.optimization_barrier((widened * gain[index]).astype(jnp.bfloat16))
        result.append(rounded.reshape(rows, heads, -1))
    return result


def local(inputs, out_grad, gains, exponent, boundary):
    block = inputs[0]
    grad_block = out_grad[0]
    gain = gains[0]
    rows, width = block.shape
    heads = exponent.shape[2]
    head_dim = width // heads
    scale = 1.0 / head_dim
    query_half, key_half, value_half = projections(block, gain, heads)
    grad_half = grad_block.reshape(rows, heads, head_dim)
    queries = query_half.astype(jnp.float32)
    key_rows = key_half.astype(jnp.float32)
    value_rows = value_half.astype(jnp.float32)
    grad_rows = grad_half.astype(jnp.float32)
    logs = decay_logs(exponent[0], boundary[0], CH).reshape(rows, heads)
    cumul = jnp.cumsum(logs, axis=0)
    growth = jnp.exp(cumul)
    tail = jnp.exp(cumul[-1][None, :] - cumul)
    forward_part = jnp.einsum(
        "shd,she->hde", key_rows * tail[:, :, None], value_rows, precision=HIGH
    )
    adjoint_part = scale * jnp.einsum(
        "shd,she->hde", queries * growth[:, :, None], grad_rows, precision=HIGH
    )
    whole_decay = jnp.exp(cumul[-1])
    cum_heads = cumul.T
    gap = cum_heads[:, :, None] - cum_heads[:, None, :]
    lower = jnp.arange(rows)[:, None] >= jnp.arange(rows)[None, :]
    decay = jnp.where(lower[None], jnp.exp(jnp.minimum(gap, 0.0)), 0.0)
    mixing = (
        jnp.einsum("thd,shd->hts", grad_half, value_half, preferred_element_type=jnp.float32)
        * decay
    )
    query_near = scale * jnp.einsum("hts,shd->thd", mixing, key_rows, precision=HIGH)
    key_near = scale * jnp.einsum("hts,thd->shd", mixing, queries, precision=HIGH)
    attention = (
        jnp.einsum("thd,shd->hts", query_half, key_half, preferred_element_type=jnp.float32) * decay
    )
    value_near = scale * jnp.einsum("hts,the->she", attention, grad_rows, precision=HIGH)
    near_total = grad_block.astype(jnp.float32)
    near_total = near_total + gain[0] * query_near.reshape(rows, width)
    near_total = near_total + gain[1] * key_near.reshape(rows, width)
    near_total = near_total + gain[2] * value_near.reshape(rows, width)
    near_round = near_total.astype(jnp.bfloat16)
    near_received = passed_along(near_round, "section", -1)
    state_in, adjoint_in, near_received = scans_in(
        forward_part, adjoint_part, whole_decay, "ctx", near_received
    )
    query_far = (
        scale * growth[:, :, None] * jnp.einsum("the,hde->thd", grad_rows, state_in, precision=HIGH)
    )
    key_far = tail[:, :, None] * jnp.einsum("she,hde->shd", value_rows, adjoint_in, precision=HIGH)
    value_far = tail[:, :, None] * jnp.einsum("shd,hde->she", key_rows, adjoint_in, precision=HIGH)
    far_total = gain[0] * query_far.reshape(rows, width)
    far_total = far_total + gain[1] * key_far.reshape(rows, width)
    far_total = far_total + gain[2] * value_far.reshape(rows, width)
    far_round = far_total.astype(jnp.bfloat16)
    far_received = passed_along(far_round, "section", -1)
    received = (near_received.astype(jnp.float32) + far_received.astype(jnp.float32)).astype(
        jnp.bfloat16
    )
    return received[None]


def solution(mesh):
    in_specs = (
        P("section", "ctx", None),
        P("section", "ctx", None),
        P("section", None, None),
        P("section", "ctx", None),
        P("section", "ctx"),
    )
    out_specs = P("section", "ctx", None)
    return jax.shard_map(local, mesh=mesh, in_specs=in_specs, out_specs=out_specs, check_vma=False)
```

```python
import math

import jax
import jax.numpy as jnp
from jax import lax
from jax.sharding import PartitionSpec as P

CH = 64


HIGH = lax.Precision.HIGHEST


def packed(state, rate):
    tile = jnp.broadcast_to(rate[:, None, None], (state.shape[0], 8, state.shape[2]))
    return jnp.concatenate([state, tile], axis=1)


def unpacked(message):
    width = message.shape[1] - 8
    return message[:, :width], message[:, width, 0]


def narrow(message):
    state, rate = unpacked(message)
    high = rate.astype(jnp.bfloat16)
    low = (rate - high.astype(jnp.float32)).astype(jnp.bfloat16)
    rows = jnp.stack([high, low] + [jnp.zeros_like(high)] * 6, axis=1)
    tile = jnp.broadcast_to(rows[:, :, None], (state.shape[0], 8, state.shape[2]))
    return jnp.concatenate([state.astype(jnp.bfloat16), tile], axis=1)


def widen(message):
    width = message.shape[1] - 8
    rate = message[:, width, 0].astype(jnp.float32) + message[:, width + 1, 0].astype(jnp.float32)
    return packed(message[:, :width].astype(jnp.float32), rate)


def sent_narrow(message, axis, pairs):
    return widen(lax.ppermute(narrow(message), axis, pairs))


def merged(farther, nearer):
    far_state, far_rate = unpacked(farther)
    near_state, near_rate = unpacked(nearer)
    return packed(near_rate[:, None, None] * far_state + near_state, far_rate * near_rate)


def both_ways(count, moves):
    return list(moves) + [(count - 1 - source, count - 1 - target) for source, target in moves]


def scans_in(forward_part, backward_part, rate, axis, held):
    count = lax.axis_size(axis)
    if count == 1:
        return jnp.zeros_like(forward_part), jnp.zeros_like(backward_part), held
    assert count % 2 == 0
    odd = lax.axis_index(axis) % 2 == 1
    couples = count // 2
    swap = [(2 * p, 2 * p + 1) for p in range(couples)] + [(2 * p + 1, 2 * p) for p in range(couples)]
    mine = jnp.where(odd, forward_part, backward_part)
    sent = packed(jnp.where(odd, backward_part, forward_part), rate)
    lower, lower_rate = unpacked(lax.ppermute(sent, axis, swap))
    window = packed(rate[:, None, None] * lower + mine, rate * lower_rate)
    if couples <= 4:
        incoming = jnp.zeros_like(mine)
        weight = jnp.ones_like(rate)
        for step in range(1, couples):
            moves = [(2 * p + 1, 2 * (p + step) + 1) for p in range(couples - step)]
            got, got_rate = unpacked(sent_narrow(window, axis, both_ways(count, moves)))
            incoming = incoming + weight[:, None, None] * got
            weight = weight * got_rate
    else:
        covered = 1
        while 2 * covered < couples:
            moves = [(2 * p + 1, 2 * (p + covered) + 1) for p in range(couples - covered)]
            window = merged(sent_narrow(window, axis, both_ways(count, moves)), window)
            covered *= 2
        moves = [(2 * p + 1, 2 * p + 3) for p in range(couples - 1)]
        nearer = sent_narrow(window, axis, both_ways(count, moves))
        if 1 + covered < couples:
            moves = [(2 * p + 1, 2 * (p + 1 + covered) + 1) for p in range(couples - 1 - covered)]
            nearer = merged(sent_narrow(window, axis, both_ways(count, moves)), nearer)
        incoming = unpacked(nearer)[0]
    incoming, held = lax.optimization_barrier((incoming, held))
    other = lax.ppermute(incoming, axis, swap)
    own = lower_rate[:, None, None] * incoming + lower
    return jnp.where(odd, own, other), jnp.where(odd, other, own), held


def passed_along(value, axis, steps):
    count = lax.axis_size(axis)
    pairs = [(source, (source + steps) % count) for source in range(count)]
    return lax.ppermute(value, axis, pairs)


def decay_logs(exponent, boundary, length):
    count, heads = exponent.shape
    rate = jnp.log(1.0 - exponent.astype(jnp.float32) / 65536.0)
    spread = jnp.broadcast_to(rate[:, None, :], (count, length, heads))
    opening = (jnp.arange(length) == 0)[None, :, None] & (boundary == 1)[:, None, None]
    return spread + jnp.where(opening, math.log(0.5), 0.0).astype(spread.dtype)


def projections(inputs, gain, heads):
    rows = inputs.shape[0]
    widened = inputs.astype(jnp.float32)
    result = []
    for index in range(3):
        rounded = lax.optimization_barrier((widened * gain[index]).astype(jnp.bfloat16))
        result.append(rounded.reshape(rows, heads, -1))
    return result


def local(inputs, out_grad, gains, exponent, boundary):
    block = inputs[0]
    grad_block = out_grad[0]
    gain = gains[0]
    rows, width = block.shape
    heads = exponent.shape[2]
    head_dim = width // heads
    scale = 1.0 / head_dim
    query_half, key_half, value_half = projections(block, gain, heads)
    grad_half = grad_block.reshape(rows, heads, head_dim)
    queries = query_half.astype(jnp.float32)
    key_rows = key_half.astype(jnp.float32)
    value_rows = value_half.astype(jnp.float32)
    grad_rows = grad_half.astype(jnp.float32)
    logs = decay_logs(exponent[0], boundary[0], CH).reshape(rows, heads)
    cumul = jnp.cumsum(logs, axis=0)
    growth = jnp.exp(cumul)
    tail = jnp.exp(cumul[-1][None, :] - cumul)
    forward_part = jnp.einsum(
        "shd,she->hde", key_rows * tail[:, :, None], value_rows, precision=HIGH
    )
    adjoint_part = scale * jnp.einsum(
        "shd,she->hde", queries * growth[:, :, None], grad_rows, precision=HIGH
    )
    whole_decay = jnp.exp(cumul[-1])
    cum_heads = cumul.T
    gap = cum_heads[:, :, None] - cum_heads[:, None, :]
    lower = jnp.arange(rows)[:, None] >= jnp.arange(rows)[None, :]
    decay = jnp.where(lower[None], jnp.exp(jnp.minimum(gap, 0.0)), 0.0)
    mixing = (
        jnp.einsum("thd,shd->hts", grad_half, value_half, preferred_element_type=jnp.float32)
        * decay
    )
    query_near = scale * jnp.einsum("hts,shd->thd", mixing, key_rows, precision=HIGH)
    key_near = scale * jnp.einsum("hts,thd->shd", mixing, queries, precision=HIGH)
    attention = (
        jnp.einsum("thd,shd->hts", query_half, key_half, preferred_element_type=jnp.float32) * decay
    )
    value_near = scale * jnp.einsum("hts,the->she", attention, grad_rows, precision=HIGH)
    near_total = grad_block.astype(jnp.float32)
    near_total = near_total + gain[0] * query_near.reshape(rows, width)
    near_total = near_total + gain[1] * key_near.reshape(rows, width)
    near_total = near_total + gain[2] * value_near.reshape(rows, width)
    near_round = near_total.astype(jnp.bfloat16)
    near_received = passed_along(near_round, "section", -1)
    state_in, adjoint_in, near_received = scans_in(
        forward_part, adjoint_part, whole_decay, "ctx", near_received
    )
    query_far = (
        scale * growth[:, :, None] * jnp.einsum("the,hde->thd", grad_rows, state_in, precision=HIGH)
    )
    key_far = tail[:, :, None] * jnp.einsum("she,hde->shd", value_rows, adjoint_in, precision=HIGH)
    value_far = tail[:, :, None] * jnp.einsum("shd,hde->she", key_rows, adjoint_in, precision=HIGH)
    far_total = gain[0] * query_far.reshape(rows, width)
    far_total = far_total + gain[1] * key_far.reshape(rows, width)
    far_total = far_total + gain[2] * value_far.reshape(rows, width)
    far_round = far_total.astype(jnp.bfloat16)
    far_received = passed_along(far_round, "section", -1)
    received = (near_received.astype(jnp.float32) + far_received.astype(jnp.float32)).astype(
        jnp.bfloat16
    )
    return received[None]


def solution(mesh):
    in_specs = (
        P("section", "ctx", None),
        P("section", "ctx", None),
        P("section", None, None),
        P("section", "ctx", None),
        P("section", "ctx"),
    )
    out_specs = P("section", "ctx", None)
    return jax.shard_map(local, mesh=mesh, in_specs=in_specs, out_specs=out_specs, check_vma=False)
```

```python
import math

import jax
import jax.numpy as jnp
from jax import lax
from jax.sharding import PartitionSpec as P

CH = 64


HIGH = lax.Precision.HIGHEST


def packed(state, rate):
    tile = jnp.broadcast_to(rate[:, None, None], (state.shape[0], 8, state.shape[2]))
    return jnp.concatenate([state, tile], axis=1)


def unpacked(message):
    width = message.shape[1] - 8
    return message[:, :width], message[:, width, 0]


def narrow(message):
    state, rate = unpacked(message)
    high = rate.astype(jnp.bfloat16)
    low = (rate - high.astype(jnp.float32)).astype(jnp.bfloat16)
    rows = jnp.stack([high, low] + [jnp.zeros_like(high)] * 6, axis=1)
    tile = jnp.broadcast_to(rows[:, :, None], (state.shape[0], 8, state.shape[2]))
    return jnp.concatenate([state.astype(jnp.bfloat16), tile], axis=1)


def widen(message):
    width = message.shape[1] - 8
    rate = message[:, width, 0].astype(jnp.float32) + message[:, width + 1, 0].astype(jnp.float32)
    return packed(message[:, :width].astype(jnp.float32), rate)


def sent_narrow(message, axis, pairs):
    return widen(lax.ppermute(narrow(message), axis, pairs))


def merged(farther, nearer):
    far_state, far_rate = unpacked(farther)
    near_state, near_rate = unpacked(nearer)
    return packed(near_rate[:, None, None] * far_state + near_state, far_rate * near_rate)


def split_dot(spec, wide, exact):
    high = wide.astype(jnp.bfloat16)
    low = (wide - high.astype(jnp.float32)).astype(jnp.bfloat16)
    first = jnp.einsum(spec, high, exact, preferred_element_type=jnp.float32)
    return first + jnp.einsum(spec, low, exact, preferred_element_type=jnp.float32)


def both_ways(count, moves):
    return list(moves) + [(count - 1 - source, count - 1 - target) for source, target in moves]


def scans_in(forward_part, backward_part, rate, axis, middle, inputs):
    count = lax.axis_size(axis)
    if count == 1:
        return jnp.zeros_like(forward_part), jnp.zeros_like(backward_part), middle(*inputs)
    assert count % 2 == 0
    odd = lax.axis_index(axis) % 2 == 1
    couples = count // 2
    swap = [(2 * p, 2 * p + 1) for p in range(couples)] + [(2 * p + 1, 2 * p) for p in range(couples)]
    mine = jnp.where(odd, forward_part, backward_part)
    sent = packed(jnp.where(odd, backward_part, forward_part), rate)
    lower, lower_rate = unpacked(lax.ppermute(sent, axis, swap))
    window = packed(rate[:, None, None] * lower + mine, rate * lower_rate)
    window, inputs = lax.optimization_barrier((window, inputs))
    held = middle(*inputs)
    if couples <= 4:
        incoming = jnp.zeros_like(mine)
        weight = jnp.ones_like(rate)
        for step in range(1, couples):
            moves = [(2 * p + 1, 2 * (p + step) + 1) for p in range(couples - step)]
            got, got_rate = unpacked(sent_narrow(window, axis, both_ways(count, moves)))
            incoming = incoming + weight[:, None, None] * got
            weight = weight * got_rate
    else:
        covered = 1
        while 2 * covered < couples:
            moves = [(2 * p + 1, 2 * (p + covered) + 1) for p in range(couples - covered)]
            window = merged(sent_narrow(window, axis, both_ways(count, moves)), window)
            covered *= 2
        moves = [(2 * p + 1, 2 * p + 3) for p in range(couples - 1)]
        nearer = sent_narrow(window, axis, both_ways(count, moves))
        if 1 + covered < couples:
            moves = [(2 * p + 1, 2 * (p + 1 + covered) + 1) for p in range(couples - 1 - covered)]
            nearer = merged(sent_narrow(window, axis, both_ways(count, moves)), nearer)
        incoming = unpacked(nearer)[0]
    incoming, held = lax.optimization_barrier((incoming, held))
    other = lax.ppermute(incoming, axis, swap)
    own = lower_rate[:, None, None] * incoming + lower
    return jnp.where(odd, own, other), jnp.where(odd, other, own), held


def passed_along(value, axis, steps):
    count = lax.axis_size(axis)
    pairs = [(source, (source + steps) % count) for source in range(count)]
    return lax.ppermute(value, axis, pairs)


def decay_logs(exponent, boundary, length):
    count, heads = exponent.shape
    rate = jnp.log(1.0 - exponent.astype(jnp.float32) / 65536.0)
    spread = jnp.broadcast_to(rate[:, None, :], (count, length, heads))
    opening = (jnp.arange(length) == 0)[None, :, None] & (boundary == 1)[:, None, None]
    return spread + jnp.where(opening, math.log(0.5), 0.0).astype(spread.dtype)


def projections(inputs, gain, heads):
    rows = inputs.shape[0]
    widened = inputs.astype(jnp.float32)
    result = []
    for index in range(3):
        rounded = lax.optimization_barrier((widened * gain[index]).astype(jnp.bfloat16))
        result.append(rounded.reshape(rows, heads, -1))
    return result


def near_terms(query_half, key_half, value_half, grad_half, cumul, grad_block, gain):
    rows, heads, head_dim = query_half.shape
    width = heads * head_dim
    scale = 1.0 / head_dim
    cum_heads = cumul.T
    gap = cum_heads[:, :, None] - cum_heads[:, None, :]
    lower = jnp.arange(rows)[:, None] >= jnp.arange(rows)[None, :]
    decay = jnp.where(lower[None], jnp.exp(jnp.minimum(gap, 0.0)), 0.0)
    mixing = (
        jnp.einsum("thd,shd->hts", grad_half, value_half, preferred_element_type=jnp.float32)
        * decay
    )
    query_near = scale * split_dot("hts,shd->thd", mixing, key_half)
    key_near = scale * split_dot("hts,thd->shd", mixing, query_half)
    attention = (
        jnp.einsum("thd,shd->hts", query_half, key_half, preferred_element_type=jnp.float32) * decay
    )
    value_near = scale * split_dot("hts,the->she", attention, grad_half)
    near_total = grad_block.astype(jnp.float32)
    near_total = near_total + gain[0] * query_near.reshape(rows, width)
    near_total = near_total + gain[1] * key_near.reshape(rows, width)
    near_total = near_total + gain[2] * value_near.reshape(rows, width)
    return passed_along(near_total.astype(jnp.bfloat16), "section", -1)


def local(inputs, out_grad, gains, exponent, boundary):
    block = inputs[0]
    grad_block = out_grad[0]
    gain = gains[0]
    rows, width = block.shape
    heads = exponent.shape[2]
    head_dim = width // heads
    scale = 1.0 / head_dim
    query_half, key_half, value_half = projections(block, gain, heads)
    grad_half = grad_block.reshape(rows, heads, head_dim)
    logs = decay_logs(exponent[0], boundary[0], CH).reshape(rows, heads)
    cumul = jnp.cumsum(logs, axis=0)
    growth = jnp.exp(cumul)
    tail = jnp.exp(cumul[-1][None, :] - cumul)
    forward_part = split_dot("shd,she->hde", key_half.astype(jnp.float32) * tail[:, :, None], value_half)
    adjoint_part = scale * split_dot(
        "shd,she->hde", query_half.astype(jnp.float32) * growth[:, :, None], grad_half
    )
    whole_decay = jnp.exp(cumul[-1])
    state_in, adjoint_in, near_received = scans_in(
        forward_part,
        adjoint_part,
        whole_decay,
        "ctx",
        near_terms,
        (query_half, key_half, value_half, grad_half, cumul, grad_block, gain),
    )
    query_far = scale * growth[:, :, None] * split_dot("hde,the->thd", state_in, grad_half)
    key_far = tail[:, :, None] * split_dot("hde,she->shd", adjoint_in, value_half)
    value_far = tail[:, :, None] * split_dot("hde,shd->she", adjoint_in, key_half)
    far_total = gain[0] * query_far.reshape(rows, width)
    far_total = far_total + gain[1] * key_far.reshape(rows, width)
    far_total = far_total + gain[2] * value_far.reshape(rows, width)
    far_received = passed_along(far_total.astype(jnp.bfloat16), "section", -1)
    received = (near_received.astype(jnp.float32) + far_received.astype(jnp.float32)).astype(
        jnp.bfloat16
    )
    return received[None]


def solution(mesh):
    in_specs = (
        P("section", "ctx", None),
        P("section", "ctx", None),
        P("section", None, None),
        P("section", "ctx", None),
        P("section", "ctx"),
    )
    out_specs = P("section", "ctx", None)
    return jax.shard_map(local, mesh=mesh, in_specs=in_specs, out_specs=out_specs, check_vma=False)
```

```python
import math

import jax
import jax.numpy as jnp
from jax import lax
from jax.sharding import PartitionSpec as P

CH = 64


HIGH = lax.Precision.HIGHEST


def packed(state, rate):
    tile = jnp.broadcast_to(rate[:, None, None], (state.shape[0], 8, state.shape[2]))
    return jnp.concatenate([state, tile], axis=1)


def unpacked(message):
    width = message.shape[1] - 8
    return message[:, :width], message[:, width, 0]


def narrow(message):
    state, rate = unpacked(message)
    high = rate.astype(jnp.bfloat16)
    low = (rate - high.astype(jnp.float32)).astype(jnp.bfloat16)
    rows = jnp.stack([high, low] + [jnp.zeros_like(high)] * 6, axis=1)
    tile = jnp.broadcast_to(rows[:, :, None], (state.shape[0], 8, state.shape[2]))
    return jnp.concatenate([state.astype(jnp.bfloat16), tile], axis=1)


def widen(message):
    width = message.shape[1] - 8
    rate = message[:, width, 0].astype(jnp.float32) + message[:, width + 1, 0].astype(jnp.float32)
    return packed(message[:, :width].astype(jnp.float32), rate)


def sent_narrow(message, axis, pairs):
    return widen(lax.ppermute(narrow(message), axis, pairs))


def merged(farther, nearer):
    far_state, far_rate = unpacked(farther)
    near_state, near_rate = unpacked(nearer)
    return packed(near_rate[:, None, None] * far_state + near_state, far_rate * near_rate)


def both_ways(count, moves):
    return list(moves) + [(count - 1 - source, count - 1 - target) for source, target in moves]


def scans_in(forward_part, backward_part, rate, axis, middle, inputs):
    count = lax.axis_size(axis)
    if count == 1:
        return jnp.zeros_like(forward_part), jnp.zeros_like(backward_part), middle(*inputs)
    assert count % 2 == 0
    odd = lax.axis_index(axis) % 2 == 1
    couples = count // 2
    swap = [(2 * p, 2 * p + 1) for p in range(couples)] + [(2 * p + 1, 2 * p) for p in range(couples)]
    mine = jnp.where(odd, forward_part, backward_part)
    sent = packed(jnp.where(odd, backward_part, forward_part), rate)
    lower, lower_rate = unpacked(lax.ppermute(sent, axis, swap))
    window = packed(rate[:, None, None] * lower + mine, rate * lower_rate)
    window, inputs = lax.optimization_barrier((window, inputs))
    held = middle(*inputs)
    if couples <= 4:
        incoming = jnp.zeros_like(mine)
        weight = jnp.ones_like(rate)
        for step in range(1, couples):
            moves = [(2 * p + 1, 2 * (p + step) + 1) for p in range(couples - step)]
            got, got_rate = unpacked(sent_narrow(window, axis, both_ways(count, moves)))
            incoming = incoming + weight[:, None, None] * got
            weight = weight * got_rate
    else:
        covered = 1
        while 2 * covered < couples:
            moves = [(2 * p + 1, 2 * (p + covered) + 1) for p in range(couples - covered)]
            window = merged(sent_narrow(window, axis, both_ways(count, moves)), window)
            covered *= 2
        moves = [(2 * p + 1, 2 * p + 3) for p in range(couples - 1)]
        nearer = sent_narrow(window, axis, both_ways(count, moves))
        if 1 + covered < couples:
            moves = [(2 * p + 1, 2 * (p + 1 + covered) + 1) for p in range(couples - 1 - covered)]
            nearer = merged(sent_narrow(window, axis, both_ways(count, moves)), nearer)
        incoming = unpacked(nearer)[0]
    incoming, held = lax.optimization_barrier((incoming, held))
    other = lax.ppermute(incoming, axis, swap)
    own = lower_rate[:, None, None] * incoming + lower
    return jnp.where(odd, own, other), jnp.where(odd, other, own), held


def passed_along(value, axis, steps):
    count = lax.axis_size(axis)
    pairs = [(source, (source + steps) % count) for source in range(count)]
    return lax.ppermute(value, axis, pairs)


def decay_logs(exponent, boundary, length):
    count, heads = exponent.shape
    rate = jnp.log(1.0 - exponent.astype(jnp.float32) / 65536.0)
    spread = jnp.broadcast_to(rate[:, None, :], (count, length, heads))
    opening = (jnp.arange(length) == 0)[None, :, None] & (boundary == 1)[:, None, None]
    return spread + jnp.where(opening, math.log(0.5), 0.0).astype(spread.dtype)


def projections(inputs, gain, heads):
    rows = inputs.shape[0]
    widened = inputs.astype(jnp.float32)
    result = []
    for index in range(3):
        rounded = lax.optimization_barrier((widened * gain[index]).astype(jnp.bfloat16))
        result.append(rounded.reshape(rows, heads, -1))
    return result


def near_terms(query_half, key_half, value_half, grad_half, cumul, grad_block, gain):
    rows, heads, head_dim = query_half.shape
    width = heads * head_dim
    scale = 1.0 / head_dim
    cum_heads = cumul.T
    gap = cum_heads[:, :, None] - cum_heads[:, None, :]
    lower = jnp.arange(rows)[:, None] >= jnp.arange(rows)[None, :]
    decay = jnp.where(lower[None], jnp.exp(jnp.minimum(gap, 0.0)), 0.0)
    mixing = (
        jnp.einsum("thd,shd->hts", grad_half, value_half, preferred_element_type=jnp.float32)
        * decay
    )
    query_near = scale * jnp.einsum("hts,shd->thd", mixing, key_half.astype(jnp.float32), precision=HIGH)
    key_near = scale * jnp.einsum("hts,thd->shd", mixing, query_half.astype(jnp.float32), precision=HIGH)
    attention = (
        jnp.einsum("thd,shd->hts", query_half, key_half, preferred_element_type=jnp.float32) * decay
    )
    value_near = scale * jnp.einsum("hts,the->she", attention, grad_half.astype(jnp.float32), precision=HIGH)
    near_total = grad_block.astype(jnp.float32)
    near_total = near_total + gain[0] * query_near.reshape(rows, width)
    near_total = near_total + gain[1] * key_near.reshape(rows, width)
    near_total = near_total + gain[2] * value_near.reshape(rows, width)
    return passed_along(near_total.astype(jnp.bfloat16), "section", -1)


def local(inputs, out_grad, gains, exponent, boundary):
    block = inputs[0]
    grad_block = out_grad[0]
    gain = gains[0]
    rows, width = block.shape
    heads = exponent.shape[2]
    head_dim = width // heads
    scale = 1.0 / head_dim
    query_half, key_half, value_half = projections(block, gain, heads)
    grad_half = grad_block.reshape(rows, heads, head_dim)
    logs = decay_logs(exponent[0], boundary[0], CH).reshape(rows, heads)
    cumul = jnp.cumsum(logs, axis=0)
    growth = jnp.exp(cumul)
    tail = jnp.exp(cumul[-1][None, :] - cumul)
    queries = query_half.astype(jnp.float32)
    key_rows = key_half.astype(jnp.float32)
    value_rows = value_half.astype(jnp.float32)
    grad_rows = grad_half.astype(jnp.float32)
    forward_part = jnp.einsum(
        "shd,she->hde", key_rows * tail[:, :, None], value_rows, precision=HIGH
    )
    adjoint_part = scale * jnp.einsum(
        "shd,she->hde", queries * growth[:, :, None], grad_rows, precision=HIGH
    )
    whole_decay = jnp.exp(cumul[-1])
    state_in, adjoint_in, near_received = scans_in(
        forward_part,
        adjoint_part,
        whole_decay,
        "ctx",
        near_terms,
        (query_half, key_half, value_half, grad_half, cumul, grad_block, gain),
    )
    query_far = (
        scale * growth[:, :, None] * jnp.einsum("the,hde->thd", grad_rows, state_in, precision=HIGH)
    )
    key_far = tail[:, :, None] * jnp.einsum("she,hde->shd", value_rows, adjoint_in, precision=HIGH)
    value_far = tail[:, :, None] * jnp.einsum("shd,hde->she", key_rows, adjoint_in, precision=HIGH)
    far_total = gain[0] * query_far.reshape(rows, width)
    far_total = far_total + gain[1] * key_far.reshape(rows, width)
    far_total = far_total + gain[2] * value_far.reshape(rows, width)
    far_received = passed_along(far_total.astype(jnp.bfloat16), "section", -1)
    received = (near_received.astype(jnp.float32) + far_received.astype(jnp.float32)).astype(
        jnp.bfloat16
    )
    return received[None]


def solution(mesh):
    in_specs = (
        P("section", "ctx", None),
        P("section", "ctx", None),
        P("section", None, None),
        P("section", "ctx", None),
        P("section", "ctx"),
    )
    out_specs = P("section", "ctx", None)
    return jax.shard_map(local, mesh=mesh, in_specs=in_specs, out_specs=out_specs, check_vma=False)
```

```python
import math

import jax
import jax.numpy as jnp
from jax import lax
from jax.sharding import PartitionSpec as P

CH = 64


HIGH = lax.Precision.HIGHEST


def packed(state, rate):
    tile = jnp.broadcast_to(rate[:, None, None], (state.shape[0], 8, state.shape[2]))
    return jnp.concatenate([state, tile], axis=1)


def unpacked(message):
    width = message.shape[1] - 8
    return message[:, :width], message[:, width, 0]


def narrow(message):
    state, rate = unpacked(message)
    high = rate.astype(jnp.bfloat16)
    low = (rate - high.astype(jnp.float32)).astype(jnp.bfloat16)
    rows = jnp.stack([high, low] + [jnp.zeros_like(high)] * 6, axis=1)
    tile = jnp.broadcast_to(rows[:, :, None], (state.shape[0], 8, state.shape[2]))
    return jnp.concatenate([state.astype(jnp.bfloat16), tile], axis=1)


def widen(message):
    width = message.shape[1] - 8
    rate = message[:, width, 0].astype(jnp.float32) + message[:, width + 1, 0].astype(jnp.float32)
    return packed(message[:, :width].astype(jnp.float32), rate)


def sent_narrow(message, axis, pairs):
    return widen(lax.ppermute(narrow(message), axis, pairs))


def merged(farther, nearer):
    far_state, far_rate = unpacked(farther)
    near_state, near_rate = unpacked(nearer)
    return packed(near_rate[:, None, None] * far_state + near_state, far_rate * near_rate)


def both_ways(count, moves):
    return list(moves) + [(count - 1 - source, count - 1 - target) for source, target in moves]


def scans_in(forward_part, backward_part, rate, axis, middle, inputs):
    count = lax.axis_size(axis)
    if count == 1:
        return jnp.zeros_like(forward_part), jnp.zeros_like(backward_part), middle(*inputs)
    assert count % 2 == 0
    odd = lax.axis_index(axis) % 2 == 1
    couples = count // 2
    swap = [(2 * p, 2 * p + 1) for p in range(couples)] + [(2 * p + 1, 2 * p) for p in range(couples)]
    mine = jnp.where(odd, forward_part, backward_part)
    sent = packed(jnp.where(odd, backward_part, forward_part), rate)
    lower, lower_rate = unpacked(lax.ppermute(sent, axis, swap))
    window = packed(rate[:, None, None] * lower + mine, rate * lower_rate)
    window, inputs = lax.optimization_barrier((window, inputs))
    held = middle(*inputs)
    if couples <= 4:
        incoming = jnp.zeros_like(mine)
        weight = jnp.ones_like(rate)
        for step in range(1, couples):
            moves = [(2 * p + 1, 2 * (p + step) + 1) for p in range(couples - step)]
            got, got_rate = unpacked(sent_narrow(window, axis, both_ways(count, moves)))
            incoming = incoming + weight[:, None, None] * got
            weight = weight * got_rate
    else:
        covered = 1
        while 2 * covered < couples:
            moves = [(2 * p + 1, 2 * (p + covered) + 1) for p in range(couples - covered)]
            window = merged(sent_narrow(window, axis, both_ways(count, moves)), window)
            covered *= 2
        moves = [(2 * p + 1, 2 * p + 3) for p in range(couples - 1)]
        nearer = sent_narrow(window, axis, both_ways(count, moves))
        if 1 + covered < couples:
            moves = [(2 * p + 1, 2 * (p + 1 + covered) + 1) for p in range(couples - 1 - covered)]
            nearer = merged(sent_narrow(window, axis, both_ways(count, moves)), nearer)
        incoming = unpacked(nearer)[0]
    other = lax.ppermute(incoming, axis, swap)
    own = lower_rate[:, None, None] * incoming + lower
    return jnp.where(odd, own, other), jnp.where(odd, other, own), held


def passed_along(value, axis, steps):
    count = lax.axis_size(axis)
    pairs = [(source, (source + steps) % count) for source in range(count)]
    return lax.ppermute(value, axis, pairs)


def decay_logs(exponent, boundary, length):
    count, heads = exponent.shape
    rate = jnp.log(1.0 - exponent.astype(jnp.float32) / 65536.0)
    spread = jnp.broadcast_to(rate[:, None, :], (count, length, heads))
    opening = (jnp.arange(length) == 0)[None, :, None] & (boundary == 1)[:, None, None]
    return spread + jnp.where(opening, math.log(0.5), 0.0).astype(spread.dtype)


def projections(inputs, gain, heads):
    rows = inputs.shape[0]
    widened = inputs.astype(jnp.float32)
    result = []
    for index in range(3):
        rounded = lax.optimization_barrier((widened * gain[index]).astype(jnp.bfloat16))
        result.append(rounded.reshape(rows, heads, -1))
    return result


def near_terms(query_half, key_half, value_half, grad_half, cumul, grad_block, gain):
    rows, heads, head_dim = query_half.shape
    width = heads * head_dim
    scale = 1.0 / head_dim
    cum_heads = cumul.T
    gap = cum_heads[:, :, None] - cum_heads[:, None, :]
    lower = jnp.arange(rows)[:, None] >= jnp.arange(rows)[None, :]
    decay = jnp.where(lower[None], jnp.exp(jnp.minimum(gap, 0.0)), 0.0)
    mixing = (
        jnp.einsum("thd,shd->hts", grad_half, value_half, preferred_element_type=jnp.float32)
        * decay
    )
    query_near = scale * jnp.einsum("hts,shd->thd", mixing, key_half.astype(jnp.float32), precision=HIGH)
    key_near = scale * jnp.einsum("hts,thd->shd", mixing, query_half.astype(jnp.float32), precision=HIGH)
    attention = (
        jnp.einsum("thd,shd->hts", query_half, key_half, preferred_element_type=jnp.float32) * decay
    )
    value_near = scale * jnp.einsum("hts,the->she", attention, grad_half.astype(jnp.float32), precision=HIGH)
    near_total = grad_block.astype(jnp.float32)
    near_total = near_total + gain[0] * query_near.reshape(rows, width)
    near_total = near_total + gain[1] * key_near.reshape(rows, width)
    near_total = near_total + gain[2] * value_near.reshape(rows, width)
    near_received = passed_along(near_total.astype(jnp.bfloat16), "section", -1)
    widened = [part.astype(jnp.float32) for part in (key_half, value_half, grad_half)]
    return near_received, widened


def local(inputs, out_grad, gains, exponent, boundary):
    block = inputs[0]
    grad_block = out_grad[0]
    gain = gains[0]
    rows, width = block.shape
    heads = exponent.shape[2]
    head_dim = width // heads
    scale = 1.0 / head_dim
    query_half, key_half, value_half = projections(block, gain, heads)
    grad_half = grad_block.reshape(rows, heads, head_dim)
    logs = decay_logs(exponent[0], boundary[0], CH).reshape(rows, heads)
    cumul = jnp.cumsum(logs, axis=0)
    growth = jnp.exp(cumul)
    tail = jnp.exp(cumul[-1][None, :] - cumul)
    queries = query_half.astype(jnp.float32)
    key_rows = key_half.astype(jnp.float32)
    value_rows = value_half.astype(jnp.float32)
    grad_rows = grad_half.astype(jnp.float32)
    forward_part = jnp.einsum(
        "shd,she->hde", key_rows * tail[:, :, None], value_rows, precision=HIGH
    )
    adjoint_part = scale * jnp.einsum(
        "shd,she->hde", queries * growth[:, :, None], grad_rows, precision=HIGH
    )
    whole_decay = jnp.exp(cumul[-1])
    state_in, adjoint_in, (near_received, widened) = scans_in(
        forward_part,
        adjoint_part,
        whole_decay,
        "ctx",
        near_terms,
        (query_half, key_half, value_half, grad_half, cumul, grad_block, gain),
    )
    key_rows, value_rows, grad_rows = widened
    query_far = (
        scale * growth[:, :, None] * jnp.einsum("the,hde->thd", grad_rows, state_in, precision=HIGH)
    )
    key_far = tail[:, :, None] * jnp.einsum("she,hde->shd", value_rows, adjoint_in, precision=HIGH)
    value_far = tail[:, :, None] * jnp.einsum("shd,hde->she", key_rows, adjoint_in, precision=HIGH)
    far_total = gain[0] * query_far.reshape(rows, width)
    far_total = far_total + gain[1] * key_far.reshape(rows, width)
    far_total = far_total + gain[2] * value_far.reshape(rows, width)
    far_received = passed_along(far_total.astype(jnp.bfloat16), "section", -1)
    received = (near_received.astype(jnp.float32) + far_received.astype(jnp.float32)).astype(
        jnp.bfloat16
    )
    return received[None]


def solution(mesh):
    in_specs = (
        P("section", "ctx", None),
        P("section", "ctx", None),
        P("section", None, None),
        P("section", "ctx", None),
        P("section", "ctx"),
    )
    out_specs = P("section", "ctx", None)
    return jax.shard_map(local, mesh=mesh, in_specs=in_specs, out_specs=out_specs, check_vma=False)
```

```python
import math

import jax
import jax.numpy as jnp
from jax import lax
from jax.sharding import PartitionSpec as P

CH = 64


HIGH = lax.Precision.HIGHEST


def packed(state, rate):
    tile = jnp.broadcast_to(rate[:, None, None], (state.shape[0], 8, state.shape[2]))
    return jnp.concatenate([state, tile], axis=1)


def unpacked(message):
    width = message.shape[1] - 8
    return message[:, :width], message[:, width, 0]


def narrow(message):
    state, rate = unpacked(message)
    high = rate.astype(jnp.bfloat16)
    low = (rate - high.astype(jnp.float32)).astype(jnp.bfloat16)
    rows = jnp.stack([high, low] + [jnp.zeros_like(high)] * 6, axis=1)
    tile = jnp.broadcast_to(rows[:, :, None], (state.shape[0], 8, state.shape[2]))
    return jnp.concatenate([state.astype(jnp.bfloat16), tile], axis=1)


def widen(message):
    width = message.shape[1] - 8
    rate = message[:, width, 0].astype(jnp.float32) + message[:, width + 1, 0].astype(jnp.float32)
    return packed(message[:, :width].astype(jnp.float32), rate)


def sent_narrow(message, axis, pairs):
    return widen(lax.ppermute(narrow(message), axis, pairs))


def merged(farther, nearer):
    far_state, far_rate = unpacked(farther)
    near_state, near_rate = unpacked(nearer)
    return packed(near_rate[:, None, None] * far_state + near_state, far_rate * near_rate)


def both_ways(count, moves):
    return list(moves) + [(count - 1 - source, count - 1 - target) for source, target in moves]


def scans_in(forward_part, backward_part, rate, axis):
    count = lax.axis_size(axis)
    if count == 1:
        return jnp.zeros_like(forward_part), jnp.zeros_like(backward_part)
    assert count % 2 == 0
    odd = lax.axis_index(axis) % 2 == 1
    couples = count // 2
    swap = [(2 * p, 2 * p + 1) for p in range(couples)] + [(2 * p + 1, 2 * p) for p in range(couples)]
    mine = jnp.where(odd, forward_part, backward_part)
    sent = packed(jnp.where(odd, backward_part, forward_part), rate)
    lower, lower_rate = unpacked(lax.ppermute(sent, axis, swap))
    window = packed(rate[:, None, None] * lower + mine, rate * lower_rate)
    if couples <= 4:
        incoming = jnp.zeros_like(mine)
        weight = jnp.ones_like(rate)
        for step in range(1, couples):
            moves = [(2 * p + 1, 2 * (p + step) + 1) for p in range(couples - step)]
            got, got_rate = unpacked(sent_narrow(window, axis, both_ways(count, moves)))
            incoming = incoming + weight[:, None, None] * got
            weight = weight * got_rate
    else:
        covered = 1
        while 2 * covered < couples:
            moves = [(2 * p + 1, 2 * (p + covered) + 1) for p in range(couples - covered)]
            window = merged(sent_narrow(window, axis, both_ways(count, moves)), window)
            covered *= 2
        moves = [(2 * p + 1, 2 * p + 3) for p in range(couples - 1)]
        nearer = sent_narrow(window, axis, both_ways(count, moves))
        if 1 + covered < couples:
            moves = [(2 * p + 1, 2 * (p + 1 + covered) + 1) for p in range(couples - 1 - covered)]
            nearer = merged(sent_narrow(window, axis, both_ways(count, moves)), nearer)
        incoming = unpacked(nearer)[0]
    other = lax.ppermute(incoming, axis, swap)
    own = lower_rate[:, None, None] * incoming + lower
    return jnp.where(odd, own, other), jnp.where(odd, other, own)


def passed_along(value, axis, steps):
    count = lax.axis_size(axis)
    pairs = [(source, (source + steps) % count) for source in range(count)]
    return lax.ppermute(value, axis, pairs)


def decay_logs(exponent, boundary, length):
    count, heads = exponent.shape
    rate = jnp.log(1.0 - exponent.astype(jnp.float32) / 65536.0)
    spread = jnp.broadcast_to(rate[:, None, :], (count, length, heads))
    opening = (jnp.arange(length) == 0)[None, :, None] & (boundary == 1)[:, None, None]
    return spread + jnp.where(opening, math.log(0.5), 0.0).astype(spread.dtype)


def projections(inputs, gain, heads):
    rows = inputs.shape[0]
    widened = inputs.astype(jnp.float32)
    result = []
    for index in range(3):
        rounded = lax.optimization_barrier((widened * gain[index]).astype(jnp.bfloat16))
        result.append(rounded.reshape(rows, heads, -1))
    return result


def near_terms(block, grad_block, gain, exponent, boundary):
    rows, width = block.shape
    heads = exponent.shape[1]
    head_dim = width // heads
    scale = 1.0 / head_dim
    query_half, key_half, value_half = projections(block, gain, heads)
    grad_half = grad_block.reshape(rows, heads, head_dim)
    queries = query_half.astype(jnp.float32)
    key_rows = key_half.astype(jnp.float32)
    grad_rows = grad_half.astype(jnp.float32)
    logs = decay_logs(exponent, boundary, CH).reshape(rows, heads)
    cumul = jnp.cumsum(logs, axis=0)
    cum_heads = cumul.T
    gap = cum_heads[:, :, None] - cum_heads[:, None, :]
    lower = jnp.arange(rows)[:, None] >= jnp.arange(rows)[None, :]
    decay = jnp.where(lower[None], jnp.exp(jnp.minimum(gap, 0.0)), 0.0)
    mixing = (
        jnp.einsum("thd,shd->hts", grad_half, value_half, preferred_element_type=jnp.float32)
        * decay
    )
    query_near = scale * jnp.einsum("hts,shd->thd", mixing, key_rows, precision=HIGH)
    key_near = scale * jnp.einsum("hts,thd->shd", mixing, queries, precision=HIGH)
    attention = (
        jnp.einsum("thd,shd->hts", query_half, key_half, preferred_element_type=jnp.float32) * decay
    )
    value_near = scale * jnp.einsum("hts,the->she", attention, grad_rows, precision=HIGH)
    near_total = grad_block.astype(jnp.float32)
    near_total = near_total + gain[0] * query_near.reshape(rows, width)
    near_total = near_total + gain[1] * key_near.reshape(rows, width)
    near_total = near_total + gain[2] * value_near.reshape(rows, width)
    return near_total.astype(jnp.bfloat16)


def far_terms(block, grad_block, gain, exponent, boundary):
    rows, width = block.shape
    heads = exponent.shape[1]
    head_dim = width // heads
    scale = 1.0 / head_dim
    query_half, key_half, value_half = projections(block, gain, heads)
    grad_half = grad_block.reshape(rows, heads, head_dim)
    queries = query_half.astype(jnp.float32)
    key_rows = key_half.astype(jnp.float32)
    value_rows = value_half.astype(jnp.float32)
    grad_rows = grad_half.astype(jnp.float32)
    logs = decay_logs(exponent, boundary, CH).reshape(rows, heads)
    cumul = jnp.cumsum(logs, axis=0)
    growth = jnp.exp(cumul)
    tail = jnp.exp(cumul[-1][None, :] - cumul)
    forward_part = jnp.einsum(
        "shd,she->hde", key_rows * tail[:, :, None], value_rows, precision=HIGH
    )
    adjoint_part = scale * jnp.einsum(
        "shd,she->hde", queries * growth[:, :, None], grad_rows, precision=HIGH
    )
    state_in, adjoint_in = scans_in(forward_part, adjoint_part, jnp.exp(cumul[-1]), "ctx")
    query_far = (
        scale * growth[:, :, None] * jnp.einsum("the,hde->thd", grad_rows, state_in, precision=HIGH)
    )
    key_far = tail[:, :, None] * jnp.einsum("she,hde->shd", value_rows, adjoint_in, precision=HIGH)
    value_far = tail[:, :, None] * jnp.einsum("shd,hde->she", key_rows, adjoint_in, precision=HIGH)
    far_total = gain[0] * query_far.reshape(rows, width)
    far_total = far_total + gain[1] * key_far.reshape(rows, width)
    far_total = far_total + gain[2] * value_far.reshape(rows, width)
    return far_total.astype(jnp.bfloat16)


def local(inputs, out_grad, gains, exponent, boundary):
    own = (inputs[0], out_grad[0], gains[0], exponent[0], boundary[0])
    small = jnp.concatenate(
        [gains[0].reshape(-1), exponent[0].reshape(-1).astype(jnp.float32), boundary[0].astype(jnp.float32)]
    )
    rows_in, small_in = passed_along((jnp.stack([inputs[0], out_grad[0]]), small), "section", -1)
    sizes = (gains[0].size, exponent[0].size)
    fetched = (
        rows_in[0],
        rows_in[1],
        small_in[: sizes[0]].reshape(gains[0].shape),
        jnp.round(small_in[sizes[0] : sizes[0] + sizes[1]]).astype(jnp.int32).reshape(exponent[0].shape),
        jnp.round(small_in[sizes[0] + sizes[1] :]).astype(jnp.int32),
    )
    near_received = passed_along(near_terms(*own), "section", -1)
    far_round = far_terms(*fetched)
    received = (near_received.astype(jnp.float32) + far_round.astype(jnp.float32)).astype(
        jnp.bfloat16
    )
    return received[None]


def solution(mesh):
    in_specs = (
        P("section", "ctx", None),
        P("section", "ctx", None),
        P("section", None, None),
        P("section", "ctx", None),
        P("section", "ctx"),
    )
    out_specs = P("section", "ctx", None)
    return jax.shard_map(local, mesh=mesh, in_specs=in_specs, out_specs=out_specs, check_vma=False)
```

```python
import math

import jax
import jax.numpy as jnp
from jax import lax
from jax.experimental.layout import Layout, with_layout_constraint
from jax.sharding import PartitionSpec as P

CH = 64


HIGH = lax.Precision.HIGHEST


def packed(state, rate):
    tile = jnp.broadcast_to(rate[:, None, None], (state.shape[0], 8, state.shape[2]))
    return jnp.concatenate([state, tile], axis=1)


def unpacked(message):
    width = message.shape[1] - 8
    return message[:, :width], message[:, width, 0]


def narrow(message):
    state, rate = unpacked(message)
    high = rate.astype(jnp.bfloat16)
    low = (rate - high.astype(jnp.float32)).astype(jnp.bfloat16)
    rows = jnp.stack([high, low] + [jnp.zeros_like(high)] * 6, axis=1)
    tile = jnp.broadcast_to(rows[:, :, None], (state.shape[0], 8, state.shape[2]))
    return jnp.concatenate([state.astype(jnp.bfloat16), tile], axis=1)


def widen(message):
    width = message.shape[1] - 8
    rate = message[:, width, 0].astype(jnp.float32) + message[:, width + 1, 0].astype(jnp.float32)
    return packed(message[:, :width].astype(jnp.float32), rate)


def sent_narrow(message, axis, pairs):
    return widen(lax.ppermute(narrow(message), axis, pairs))


def merged(farther, nearer):
    far_state, far_rate = unpacked(farther)
    near_state, near_rate = unpacked(nearer)
    return packed(near_rate[:, None, None] * far_state + near_state, far_rate * near_rate)


def both_ways(count, moves):
    return list(moves) + [(count - 1 - source, count - 1 - target) for source, target in moves]


def scans_in(forward_part, backward_part, rate, axis, held):
    count = lax.axis_size(axis)
    if count == 1:
        return jnp.zeros_like(forward_part), jnp.zeros_like(backward_part), held
    assert count % 2 == 0
    odd = lax.axis_index(axis) % 2 == 1
    couples = count // 2
    swap = [(2 * p, 2 * p + 1) for p in range(couples)] + [(2 * p + 1, 2 * p) for p in range(couples)]
    mine = jnp.where(odd, forward_part, backward_part)
    sent = packed(jnp.where(odd, backward_part, forward_part), rate)
    lower, lower_rate = unpacked(lax.ppermute(sent, axis, swap))
    window = packed(rate[:, None, None] * lower + mine, rate * lower_rate)
    window, held = lax.optimization_barrier((window, held))
    if couples <= 4:
        incoming = jnp.zeros_like(mine)
        weight = jnp.ones_like(rate)
        for step in range(1, couples):
            moves = [(2 * p + 1, 2 * (p + step) + 1) for p in range(couples - step)]
            got, got_rate = unpacked(sent_narrow(window, axis, both_ways(count, moves)))
            incoming = incoming + weight[:, None, None] * got
            weight = weight * got_rate
    else:
        covered = 1
        while 2 * covered < couples:
            moves = [(2 * p + 1, 2 * (p + covered) + 1) for p in range(couples - covered)]
            window = merged(sent_narrow(window, axis, both_ways(count, moves)), window)
            covered *= 2
        moves = [(2 * p + 1, 2 * p + 3) for p in range(couples - 1)]
        nearer = sent_narrow(window, axis, both_ways(count, moves))
        if 1 + covered < couples:
            moves = [(2 * p + 1, 2 * (p + 1 + covered) + 1) for p in range(couples - 1 - covered)]
            nearer = merged(sent_narrow(window, axis, both_ways(count, moves)), nearer)
        incoming = unpacked(nearer)[0]
    other = lax.ppermute(incoming, axis, swap)
    own = lower_rate[:, None, None] * incoming + lower
    return jnp.where(odd, own, other), jnp.where(odd, other, own), held


def passed_along(value, axis, steps):
    count = lax.axis_size(axis)
    pairs = [(source, (source + steps) % count) for source in range(count)]
    return lax.ppermute(value, axis, pairs)


def decay_logs(exponent, boundary, length):
    count, heads = exponent.shape
    rate = jnp.log(1.0 - exponent.astype(jnp.float32) / 65536.0)
    spread = jnp.broadcast_to(rate[:, None, :], (count, length, heads))
    opening = (jnp.arange(length) == 0)[None, :, None] & (boundary == 1)[:, None, None]
    return spread + jnp.where(opening, math.log(0.5), 0.0).astype(spread.dtype)


def projections(inputs, gain, heads):
    rows = inputs.shape[0]
    widened = inputs.astype(jnp.float32)
    result = []
    for index in range(3):
        rounded = lax.optimization_barrier((widened * gain[index]).astype(jnp.bfloat16))
        result.append(rounded.reshape(rows, heads, -1))
    return result


def local(inputs, out_grad, gains, exponent, boundary):
    block = inputs[0]
    grad_block = out_grad[0]
    gain = gains[0]
    rows, width = block.shape
    heads = exponent.shape[2]
    head_dim = width // heads
    scale = 1.0 / head_dim
    query_half, key_half, value_half = projections(block, gain, heads)
    grad_half = grad_block.reshape(rows, heads, head_dim)
    queries = query_half.astype(jnp.float32)
    key_rows = key_half.astype(jnp.float32)
    value_rows = value_half.astype(jnp.float32)
    grad_rows = grad_half.astype(jnp.float32)
    logs = decay_logs(exponent[0], boundary[0], CH).reshape(rows, heads)
    cumul = jnp.cumsum(logs, axis=0)
    growth = jnp.exp(cumul)
    tail = jnp.exp(cumul[-1][None, :] - cumul)
    forward_part = jnp.einsum(
        "shd,she->hde", key_rows * tail[:, :, None], value_rows, precision=HIGH
    )
    adjoint_part = scale * jnp.einsum(
        "shd,she->hde", queries * growth[:, :, None], grad_rows, precision=HIGH
    )
    whole_decay = jnp.exp(cumul[-1])
    state_in, adjoint_in, held = scans_in(
        forward_part, adjoint_part, whole_decay, "ctx", (query_half, key_half, value_half, grad_half)
    )
    query_half, key_half, value_half, grad_half = held
    queries = query_half.astype(jnp.float32)
    key_rows = key_half.astype(jnp.float32)
    value_rows = value_half.astype(jnp.float32)
    grad_rows = grad_half.astype(jnp.float32)
    cum_heads = cumul.T
    gap = cum_heads[:, :, None] - cum_heads[:, None, :]
    lower = jnp.arange(rows)[:, None] >= jnp.arange(rows)[None, :]
    decay = jnp.where(lower[None], jnp.exp(jnp.minimum(gap, 0.0)), 0.0)
    mixing = (
        jnp.einsum("thd,shd->hts", grad_half, value_half, preferred_element_type=jnp.float32)
        * decay
    )
    query_near = scale * jnp.einsum("hts,shd->thd", mixing, key_rows, precision=HIGH)
    key_near = scale * jnp.einsum("hts,thd->shd", mixing, queries, precision=HIGH)
    attention = (
        jnp.einsum("thd,shd->hts", query_half, key_half, preferred_element_type=jnp.float32) * decay
    )
    value_near = scale * jnp.einsum("hts,the->she", attention, grad_rows, precision=HIGH)
    near_total = grad_block.astype(jnp.float32)
    near_total = near_total + gain[0] * query_near.reshape(rows, width)
    near_total = near_total + gain[1] * key_near.reshape(rows, width)
    near_total = near_total + gain[2] * value_near.reshape(rows, width)
    near_round = with_layout_constraint(near_total.astype(jnp.bfloat16), Layout((1, 0)))
    near_received = passed_along(near_round, "section", -1)
    near_received, state_in, adjoint_in = lax.optimization_barrier(
        (near_received, state_in, adjoint_in)
    )
    query_far = (
        scale * growth[:, :, None] * jnp.einsum("the,hde->thd", grad_rows, state_in, precision=HIGH)
    )
    key_far = tail[:, :, None] * jnp.einsum("she,hde->shd", value_rows, adjoint_in, precision=HIGH)
    value_far = tail[:, :, None] * jnp.einsum("shd,hde->she", key_rows, adjoint_in, precision=HIGH)
    far_total = gain[0] * query_far.reshape(rows, width)
    far_total = far_total + gain[1] * key_far.reshape(rows, width)
    far_total = far_total + gain[2] * value_far.reshape(rows, width)
    far_round = with_layout_constraint(far_total.astype(jnp.bfloat16), Layout((1, 0)))
    far_received = passed_along(far_round, "section", -1)
    received = (near_received.astype(jnp.float32) + far_received.astype(jnp.float32)).astype(
        jnp.bfloat16
    )
    return received[None]


def solution(mesh):
    in_specs = (
        P("section", "ctx", None),
        P("section", "ctx", None),
        P("section", None, None),
        P("section", "ctx", None),
        P("section", "ctx"),
    )
    out_specs = P("section", "ctx", None)
    return jax.shard_map(local, mesh=mesh, in_specs=in_specs, out_specs=out_specs, check_vma=False)
```

```python
import math

import jax
import jax.numpy as jnp
from jax import lax
from jax.experimental.layout import Layout, with_layout_constraint
from jax.sharding import PartitionSpec as P

CH = 64


HIGH = lax.Precision.HIGHEST


def packed(state, rate):
    tile = jnp.broadcast_to(rate[:, None, None], (state.shape[0], 8, state.shape[2]))
    return jnp.concatenate([state, tile], axis=1)


def unpacked(message):
    width = message.shape[1] - 8
    return message[:, :width], message[:, width, 0]


def narrow(message):
    state, rate = unpacked(message)
    high = rate.astype(jnp.bfloat16)
    low = (rate - high.astype(jnp.float32)).astype(jnp.bfloat16)
    rows = jnp.stack([high, low] + [jnp.zeros_like(high)] * 6, axis=1)
    tile = jnp.broadcast_to(rows[:, :, None], (state.shape[0], 8, state.shape[2]))
    return jnp.concatenate([state.astype(jnp.bfloat16), tile], axis=1)


def widen(message):
    width = message.shape[1] - 8
    rate = message[:, width, 0].astype(jnp.float32) + message[:, width + 1, 0].astype(jnp.float32)
    return packed(message[:, :width].astype(jnp.float32), rate)


def sent_narrow(message, axis, pairs):
    return widen(lax.ppermute(narrow(message), axis, pairs))


def merged(farther, nearer):
    far_state, far_rate = unpacked(farther)
    near_state, near_rate = unpacked(nearer)
    return packed(near_rate[:, None, None] * far_state + near_state, far_rate * near_rate)


def both_ways(count, moves):
    return list(moves) + [(count - 1 - source, count - 1 - target) for source, target in moves]


def scans_in(forward_part, backward_part, rate, axis, held, middle):
    count = lax.axis_size(axis)
    if count == 1:
        return jnp.zeros_like(forward_part), jnp.zeros_like(backward_part), middle(*held)
    assert count % 2 == 0
    odd = lax.axis_index(axis) % 2 == 1
    couples = count // 2
    swap = [(2 * p, 2 * p + 1) for p in range(couples)] + [(2 * p + 1, 2 * p) for p in range(couples)]
    mine = jnp.where(odd, forward_part, backward_part)
    sent = packed(jnp.where(odd, backward_part, forward_part), rate)
    lower, lower_rate = unpacked(lax.ppermute(sent, axis, swap))
    window = packed(rate[:, None, None] * lower + mine, rate * lower_rate)
    window, held = lax.optimization_barrier((window, held))
    if couples <= 4:
        arrived = []
        for step in range(1, couples):
            moves = [(2 * p + 1, 2 * (p + step) + 1) for p in range(couples - step)]
            arrived.append(lax.ppermute(narrow(window), axis, both_ways(count, moves)))
        made = middle(*held)
        arrived, made = lax.optimization_barrier((arrived, made))
        incoming = jnp.zeros_like(mine)
        weight = jnp.ones_like(rate)
        for message in arrived:
            got, got_rate = unpacked(widen(message))
            incoming = incoming + weight[:, None, None] * got
            weight = weight * got_rate
    else:
        made = middle(*held)
        covered = 1
        while 2 * covered < couples:
            moves = [(2 * p + 1, 2 * (p + covered) + 1) for p in range(couples - covered)]
            window = merged(sent_narrow(window, axis, both_ways(count, moves)), window)
            covered *= 2
        moves = [(2 * p + 1, 2 * p + 3) for p in range(couples - 1)]
        nearer = sent_narrow(window, axis, both_ways(count, moves))
        if 1 + covered < couples:
            moves = [(2 * p + 1, 2 * (p + 1 + covered) + 1) for p in range(couples - 1 - covered)]
            nearer = merged(sent_narrow(window, axis, both_ways(count, moves)), nearer)
        incoming = unpacked(nearer)[0]
    other = lax.ppermute(incoming, axis, swap)
    own = lower_rate[:, None, None] * incoming + lower
    return jnp.where(odd, own, other), jnp.where(odd, other, own), made


def passed_along(value, axis, steps):
    count = lax.axis_size(axis)
    pairs = [(source, (source + steps) % count) for source in range(count)]
    return lax.ppermute(value, axis, pairs)


def decay_logs(exponent, boundary, length):
    count, heads = exponent.shape
    rate = jnp.log(1.0 - exponent.astype(jnp.float32) / 65536.0)
    spread = jnp.broadcast_to(rate[:, None, :], (count, length, heads))
    opening = (jnp.arange(length) == 0)[None, :, None] & (boundary == 1)[:, None, None]
    return spread + jnp.where(opening, math.log(0.5), 0.0).astype(spread.dtype)


def projections(inputs, gain, heads):
    rows = inputs.shape[0]
    widened = inputs.astype(jnp.float32)
    result = []
    for index in range(3):
        rounded = lax.optimization_barrier((widened * gain[index]).astype(jnp.bfloat16))
        result.append(rounded.reshape(rows, heads, -1))
    return result


def near_terms(query_half, key_half, value_half, grad_half, cumul, grad_block, gain):
    rows, heads, head_dim = query_half.shape
    width = heads * head_dim
    scale = 1.0 / head_dim
    queries = query_half.astype(jnp.float32)
    key_rows = key_half.astype(jnp.float32)
    grad_rows = grad_half.astype(jnp.float32)
    cum_heads = cumul.T
    gap = cum_heads[:, :, None] - cum_heads[:, None, :]
    lower = jnp.arange(rows)[:, None] >= jnp.arange(rows)[None, :]
    decay = jnp.where(lower[None], jnp.exp(jnp.minimum(gap, 0.0)), 0.0)
    mixing = (
        jnp.einsum("thd,shd->hts", grad_half, value_half, preferred_element_type=jnp.float32)
        * decay
    )
    query_near = scale * jnp.einsum("hts,shd->thd", mixing, key_rows, precision=HIGH)
    key_near = scale * jnp.einsum("hts,thd->shd", mixing, queries, precision=HIGH)
    attention = (
        jnp.einsum("thd,shd->hts", query_half, key_half, preferred_element_type=jnp.float32) * decay
    )
    value_near = scale * jnp.einsum("hts,the->she", attention, grad_rows, precision=HIGH)
    near_total = grad_block.astype(jnp.float32)
    near_total = near_total + gain[0] * query_near.reshape(rows, width)
    near_total = near_total + gain[1] * key_near.reshape(rows, width)
    near_total = near_total + gain[2] * value_near.reshape(rows, width)
    near_round = with_layout_constraint(near_total.astype(jnp.bfloat16), Layout((1, 0)))
    return passed_along(near_round, "section", -1)


def local(inputs, out_grad, gains, exponent, boundary):
    block = inputs[0]
    grad_block = out_grad[0]
    gain = gains[0]
    rows, width = block.shape
    heads = exponent.shape[2]
    head_dim = width // heads
    scale = 1.0 / head_dim
    query_half, key_half, value_half = projections(block, gain, heads)
    grad_half = grad_block.reshape(rows, heads, head_dim)
    queries = query_half.astype(jnp.float32)
    key_rows = key_half.astype(jnp.float32)
    value_rows = value_half.astype(jnp.float32)
    grad_rows = grad_half.astype(jnp.float32)
    logs = decay_logs(exponent[0], boundary[0], CH).reshape(rows, heads)
    cumul = jnp.cumsum(logs, axis=0)
    growth = jnp.exp(cumul)
    tail = jnp.exp(cumul[-1][None, :] - cumul)
    forward_part = jnp.einsum(
        "shd,she->hde", key_rows * tail[:, :, None], value_rows, precision=HIGH
    )
    adjoint_part = scale * jnp.einsum(
        "shd,she->hde", queries * growth[:, :, None], grad_rows, precision=HIGH
    )
    whole_decay = jnp.exp(cumul[-1])
    state_in, adjoint_in, near_received = scans_in(
        forward_part,
        adjoint_part,
        whole_decay,
        "ctx",
        (query_half, key_half, value_half, grad_half, cumul, grad_block, gain),
        near_terms,
    )
    query_far = (
        scale * growth[:, :, None] * jnp.einsum("the,hde->thd", grad_rows, state_in, precision=HIGH)
    )
    key_far = tail[:, :, None] * jnp.einsum("she,hde->shd", value_rows, adjoint_in, precision=HIGH)
    value_far = tail[:, :, None] * jnp.einsum("shd,hde->she", key_rows, adjoint_in, precision=HIGH)
    far_total = gain[0] * query_far.reshape(rows, width)
    far_total = far_total + gain[1] * key_far.reshape(rows, width)
    far_total = far_total + gain[2] * value_far.reshape(rows, width)
    far_round = with_layout_constraint(far_total.astype(jnp.bfloat16), Layout((1, 0)))
    far_received = passed_along(far_round, "section", -1)
    received = (near_received.astype(jnp.float32) + far_received.astype(jnp.float32)).astype(
        jnp.bfloat16
    )
    return received[None]


def solution(mesh):
    in_specs = (
        P("section", "ctx", None),
        P("section", "ctx", None),
        P("section", None, None),
        P("section", "ctx", None),
        P("section", "ctx"),
    )
    out_specs = P("section", "ctx", None)
    return jax.shard_map(local, mesh=mesh, in_specs=in_specs, out_specs=out_specs, check_vma=False)
```

```python
import math

import jax
import jax.numpy as jnp
from jax import lax
from jax.sharding import PartitionSpec as P

CH = 64


HIGH = lax.Precision.HIGHEST


def packed(state, rate):
    tile = jnp.broadcast_to(rate[:, None, None], (state.shape[0], 8, state.shape[2]))
    return jnp.concatenate([state, tile], axis=1)


def unpacked(message):
    width = message.shape[1] - 8
    return message[:, :width], message[:, width, 0]


def narrow(message):
    state, rate = unpacked(message)
    high = rate.astype(jnp.bfloat16)
    low = (rate - high.astype(jnp.float32)).astype(jnp.bfloat16)
    rows = jnp.stack([high, low] + [jnp.zeros_like(high)] * 6, axis=1)
    tile = jnp.broadcast_to(rows[:, :, None], (state.shape[0], 8, state.shape[2]))
    return jnp.concatenate([state.astype(jnp.bfloat16), tile], axis=1)


def widen(message):
    width = message.shape[1] - 8
    rate = message[:, width, 0].astype(jnp.float32) + message[:, width + 1, 0].astype(jnp.float32)
    return packed(message[:, :width].astype(jnp.float32), rate)


def sent_narrow(message, axis, pairs):
    return widen(lax.ppermute(narrow(message), axis, pairs))


def merged(farther, nearer):
    far_state, far_rate = unpacked(farther)
    near_state, near_rate = unpacked(nearer)
    return packed(near_rate[:, None, None] * far_state + near_state, far_rate * near_rate)


def both_ways(count, moves):
    return list(moves) + [(count - 1 - source, count - 1 - target) for source, target in moves]


def table(values, index):
    return jnp.asarray(values, jnp.float32)[index]


def scans_four(forward_part, backward_part, rate, axis):
    here = lax.axis_index(axis)
    odd = here % 2 == 1
    swap = [(2 * p, 2 * p + 1) for p in range(4)] + [(2 * p + 1, 2 * p) for p in range(4)]
    mine = jnp.stack([packed(forward_part, rate), packed(backward_part, rate)])
    theirs = lax.ppermute(mine, axis, swap)
    even_forward, even_rate = unpacked(jnp.where(odd, theirs[0], mine[0]))
    odd_forward, odd_rate = unpacked(jnp.where(odd, mine[0], theirs[0]))
    even_backward = unpacked(jnp.where(odd, theirs[1], mine[1]))[0]
    odd_backward = unpacked(jnp.where(odd, mine[1], theirs[1]))[0]
    both_rate = even_rate * odd_rate
    ahead = packed(odd_rate[:, None, None] * even_forward + odd_forward, both_rate)
    behind = packed(even_rate[:, None, None] * odd_backward + even_backward, both_rate)
    first_pairs = [(0, 2), (1, 5), (2, 0), (3, 7), (4, 3), (5, 6), (6, 4), (7, 1)]
    second_pairs = [(0, 7), (2, 4), (4, 1), (6, 2)]
    first_sent = jnp.where(table([1, 1, 0, 1, 0, 1, 0, 0], here) > 0, ahead, behind)
    second_sent = jnp.where(table([1, 0, 1, 0, 0, 0, 0, 0], here) > 0, ahead, behind)
    one, one_rate = unpacked(widen(lax.ppermute(narrow(first_sent), axis, first_pairs)))
    two, two_rate = unpacked(widen(lax.ppermute(narrow(second_sent), axis, second_pairs)))

    def partial(c_one, c_two, c_one_two, c_two_one, r_one, r_two):
        value = (
            table(c_one, here) * one
            + table(c_two, here) * two
            + (table(c_one_two, here) * one_rate)[:, None, None] * two
            + (table(c_two_one, here) * two_rate)[:, None, None] * one
        )
        kept = table(r_one, here) * one_rate + table(r_two, here) * two_rate
        kept = kept + (1.0 - table(r_one, here) - table(r_two, here))
        return packed(value, kept)

    forward_partial = partial(
        [0, 0, 1, 0, 0, 1, 1, 1], [0, 0, 0, 0, 1, 0, 0, 0], [0, 0, 0, 0, 0, 0, 0, 1],
        [0] * 8, [0, 0, 1, 0, 0, 0, 1, 0], [0, 0, 0, 0, 1, 0, 0, 0],
    )
    backward_partial = partial(
        [1, 0, 0, 1, 1, 0, 0, 0], [0, 1, 1, 0, 0, 0, 0, 0], [0] * 8,
        [0, 1, 0, 0, 0, 0, 0, 0], [1, 0, 0, 1, 1, 0, 0, 0], [0] * 8,
    )
    own = jnp.stack([forward_partial, backward_partial])
    other = lax.ppermute(own, axis, swap)

    def joined(position, near_flags):
        near = table(near_flags, here) > 0
        near_value, near_rate = unpacked(jnp.where(near, own[position], other[position]))
        far_value = unpacked(jnp.where(near, other[position], own[position]))[0]
        return near_value + near_rate[:, None, None] * far_value

    forward_in = joined(0, [1, 0, 1, 0, 1, 0, 1, 0])
    backward_in = joined(1, [1, 0, 0, 1, 1, 0, 1, 0])
    state_in = jnp.where(odd, even_rate[:, None, None] * forward_in + even_forward, forward_in)
    adjoint_in = jnp.where(odd, backward_in, odd_rate[:, None, None] * backward_in + odd_backward)
    return state_in, adjoint_in


def scans_in(forward_part, backward_part, rate, axis, held):
    count = lax.axis_size(axis)
    if count == 1:
        return jnp.zeros_like(forward_part), jnp.zeros_like(backward_part), held
    assert count % 2 == 0
    if count == 8:
        return scans_four(forward_part, backward_part, rate, axis) + (held,)
    odd = lax.axis_index(axis) % 2 == 1
    couples = count // 2
    swap = [(2 * p, 2 * p + 1) for p in range(couples)] + [(2 * p + 1, 2 * p) for p in range(couples)]
    mine = jnp.where(odd, forward_part, backward_part)
    sent = packed(jnp.where(odd, backward_part, forward_part), rate)
    lower, lower_rate = unpacked(lax.ppermute(sent, axis, swap))
    window = packed(rate[:, None, None] * lower + mine, rate * lower_rate)
    if couples <= 4:
        incoming = jnp.zeros_like(mine)
        weight = jnp.ones_like(rate)
        for step in range(1, couples):
            moves = [(2 * p + 1, 2 * (p + step) + 1) for p in range(couples - step)]
            got, got_rate = unpacked(sent_narrow(window, axis, both_ways(count, moves)))
            incoming = incoming + weight[:, None, None] * got
            weight = weight * got_rate
    else:
        covered = 1
        while 2 * covered < couples:
            moves = [(2 * p + 1, 2 * (p + covered) + 1) for p in range(couples - covered)]
            window = merged(sent_narrow(window, axis, both_ways(count, moves)), window)
            covered *= 2
        moves = [(2 * p + 1, 2 * p + 3) for p in range(couples - 1)]
        nearer = sent_narrow(window, axis, both_ways(count, moves))
        if 1 + covered < couples:
            moves = [(2 * p + 1, 2 * (p + 1 + covered) + 1) for p in range(couples - 1 - covered)]
            nearer = merged(sent_narrow(window, axis, both_ways(count, moves)), nearer)
        incoming = unpacked(nearer)[0]
    incoming, held = lax.optimization_barrier((incoming, held))
    other = lax.ppermute(incoming, axis, swap)
    own = lower_rate[:, None, None] * incoming + lower
    return jnp.where(odd, own, other), jnp.where(odd, other, own), held


def passed_along(value, axis, steps):
    count = lax.axis_size(axis)
    pairs = [(source, (source + steps) % count) for source in range(count)]
    return lax.ppermute(value, axis, pairs)


def decay_logs(exponent, boundary, length):
    count, heads = exponent.shape
    rate = jnp.log(1.0 - exponent.astype(jnp.float32) / 65536.0)
    spread = jnp.broadcast_to(rate[:, None, :], (count, length, heads))
    opening = (jnp.arange(length) == 0)[None, :, None] & (boundary == 1)[:, None, None]
    return spread + jnp.where(opening, math.log(0.5), 0.0).astype(spread.dtype)


def projections(inputs, gain, heads):
    rows = inputs.shape[0]
    widened = inputs.astype(jnp.float32)
    result = []
    for index in range(3):
        rounded = lax.optimization_barrier((widened * gain[index]).astype(jnp.bfloat16))
        result.append(rounded.reshape(rows, heads, -1))
    return result


def local(inputs, out_grad, gains, exponent, boundary):
    block = inputs[0]
    grad_block = out_grad[0]
    gain = gains[0]
    rows, width = block.shape
    heads = exponent.shape[2]
    head_dim = width // heads
    scale = 1.0 / head_dim
    query_half, key_half, value_half = projections(block, gain, heads)
    grad_half = grad_block.reshape(rows, heads, head_dim)
    queries = query_half.astype(jnp.float32)
    key_rows = key_half.astype(jnp.float32)
    value_rows = value_half.astype(jnp.float32)
    grad_rows = grad_half.astype(jnp.float32)
    logs = decay_logs(exponent[0], boundary[0], CH).reshape(rows, heads)
    cumul = jnp.cumsum(logs, axis=0)
    growth = jnp.exp(cumul)
    tail = jnp.exp(cumul[-1][None, :] - cumul)
    forward_part = jnp.einsum(
        "shd,she->hde", key_rows * tail[:, :, None], value_rows, precision=HIGH
    )
    adjoint_part = scale * jnp.einsum(
        "shd,she->hde", queries * growth[:, :, None], grad_rows, precision=HIGH
    )
    whole_decay = jnp.exp(cumul[-1])
    cum_heads = cumul.T
    gap = cum_heads[:, :, None] - cum_heads[:, None, :]
    lower = jnp.arange(rows)[:, None] >= jnp.arange(rows)[None, :]
    decay = jnp.where(lower[None], jnp.exp(jnp.minimum(gap, 0.0)), 0.0)
    mixing = (
        jnp.einsum("thd,shd->hts", grad_half, value_half, preferred_element_type=jnp.float32)
        * decay
    )
    query_near = scale * jnp.einsum("hts,shd->thd", mixing, key_rows, precision=HIGH)
    key_near = scale * jnp.einsum("hts,thd->shd", mixing, queries, precision=HIGH)
    attention = (
        jnp.einsum("thd,shd->hts", query_half, key_half, preferred_element_type=jnp.float32) * decay
    )
    value_near = scale * jnp.einsum("hts,the->she", attention, grad_rows, precision=HIGH)
    near_total = grad_block.astype(jnp.float32)
    near_total = near_total + gain[0] * query_near.reshape(rows, width)
    near_total = near_total + gain[1] * key_near.reshape(rows, width)
    near_total = near_total + gain[2] * value_near.reshape(rows, width)
    near_round = near_total.astype(jnp.bfloat16)
    near_received = passed_along(near_round, "section", -1)
    state_in, adjoint_in, near_received = scans_in(
        forward_part, adjoint_part, whole_decay, "ctx", near_received
    )
    query_far = (
        scale * growth[:, :, None] * jnp.einsum("the,hde->thd", grad_rows, state_in, precision=HIGH)
    )
    key_far = tail[:, :, None] * jnp.einsum("she,hde->shd", value_rows, adjoint_in, precision=HIGH)
    value_far = tail[:, :, None] * jnp.einsum("shd,hde->she", key_rows, adjoint_in, precision=HIGH)
    far_total = gain[0] * query_far.reshape(rows, width)
    far_total = far_total + gain[1] * key_far.reshape(rows, width)
    far_total = far_total + gain[2] * value_far.reshape(rows, width)
    far_round = far_total.astype(jnp.bfloat16)
    far_received = passed_along(far_round, "section", -1)
    received = (near_received.astype(jnp.float32) + far_received.astype(jnp.float32)).astype(
        jnp.bfloat16
    )
    return received[None]


def solution(mesh):
    in_specs = (
        P("section", "ctx", None),
        P("section", "ctx", None),
        P("section", None, None),
        P("section", "ctx", None),
        P("section", "ctx"),
    )
    out_specs = P("section", "ctx", None)
    return jax.shard_map(local, mesh=mesh, in_specs=in_specs, out_specs=out_specs, check_vma=False)
```

```python
import math

import jax
import jax.numpy as jnp
from jax import lax
from jax.sharding import PartitionSpec as P

CH = 64


HIGH = lax.Precision.HIGHEST


def packed(state, rate):
    tile = jnp.broadcast_to(rate[:, None, None], (state.shape[0], 8, state.shape[2]))
    return jnp.concatenate([state, tile], axis=1)


def unpacked(message):
    width = message.shape[1] - 8
    return message[:, :width], message[:, width, 0]


def narrow(message):
    state, rate = unpacked(message)
    high = rate.astype(jnp.bfloat16)
    low = (rate - high.astype(jnp.float32)).astype(jnp.bfloat16)
    rows = jnp.stack([high, low] + [jnp.zeros_like(high)] * 6, axis=1)
    tile = jnp.broadcast_to(rows[:, :, None], (state.shape[0], 8, state.shape[2]))
    return jnp.concatenate([state.astype(jnp.bfloat16), tile], axis=1)


def widen(message):
    width = message.shape[1] - 8
    rate = message[:, width, 0].astype(jnp.float32) + message[:, width + 1, 0].astype(jnp.float32)
    return packed(message[:, :width].astype(jnp.float32), rate)


def sent_narrow(message, axis, pairs):
    return widen(lax.ppermute(narrow(message), axis, pairs))


def merged(farther, nearer):
    far_state, far_rate = unpacked(farther)
    near_state, near_rate = unpacked(nearer)
    return packed(near_rate[:, None, None] * far_state + near_state, far_rate * near_rate)


def both_ways(count, moves):
    return list(moves) + [(count - 1 - source, count - 1 - target) for source, target in moves]


def scans_in(forward_part, backward_part, rate, axis, held):
    count = lax.axis_size(axis)
    if count == 1:
        return jnp.zeros_like(forward_part), jnp.zeros_like(backward_part), held
    assert count % 2 == 0
    odd = lax.axis_index(axis) % 2 == 1
    couples = count // 2
    swap = [(2 * p, 2 * p + 1) for p in range(couples)] + [(2 * p + 1, 2 * p) for p in range(couples)]
    mine = jnp.where(odd, forward_part, backward_part)
    sent = packed(jnp.where(odd, backward_part, forward_part), rate)
    lower, lower_rate = unpacked(lax.ppermute(sent, axis, swap))
    window = packed(rate[:, None, None] * lower + mine, rate * lower_rate)
    if couples <= 4:
        incoming = jnp.zeros_like(mine)
        weight = jnp.ones_like(rate)
        for step in range(1, couples):
            moves = [(2 * p + 1, 2 * (p + step) + 1) for p in range(couples - step)]
            got, got_rate = unpacked(sent_narrow(window, axis, both_ways(count, moves)))
            incoming = incoming + weight[:, None, None] * got
            weight = weight * got_rate
    else:
        covered = 1
        while 2 * covered < couples:
            moves = [(2 * p + 1, 2 * (p + covered) + 1) for p in range(couples - covered)]
            window = merged(sent_narrow(window, axis, both_ways(count, moves)), window)
            covered *= 2
        moves = [(2 * p + 1, 2 * p + 3) for p in range(couples - 1)]
        nearer = sent_narrow(window, axis, both_ways(count, moves))
        if 1 + covered < couples:
            moves = [(2 * p + 1, 2 * (p + 1 + covered) + 1) for p in range(couples - 1 - covered)]
            nearer = merged(sent_narrow(window, axis, both_ways(count, moves)), nearer)
        incoming = unpacked(nearer)[0]
    incoming, held = lax.optimization_barrier((incoming, held))
    other = lax.ppermute(incoming, axis, swap)
    own = lower_rate[:, None, None] * incoming + lower
    return jnp.where(odd, own, other), jnp.where(odd, other, own), held


def passed_along(value, axis, steps):
    count = lax.axis_size(axis)
    pairs = [(source, (source + steps) % count) for source in range(count)]
    straight = [pair for pair in pairs if abs(pair[1] - pair[0]) == abs(steps)]
    wrapped = [pair for pair in pairs if abs(pair[1] - pair[0]) != abs(steps)]
    if not straight or not wrapped:
        return lax.ppermute(value, axis, pairs)
    near = lax.ppermute(value, axis, straight)
    far = lax.ppermute(value, axis, wrapped)
    here = lax.axis_index(axis)
    takes_wrapped = (here - steps < 0) | (here - steps >= count)
    return jax.tree.map(lambda a, b: jnp.where(takes_wrapped, b, a), near, far)


def decay_logs(exponent, boundary, length):
    count, heads = exponent.shape
    rate = jnp.log(1.0 - exponent.astype(jnp.float32) / 65536.0)
    spread = jnp.broadcast_to(rate[:, None, :], (count, length, heads))
    opening = (jnp.arange(length) == 0)[None, :, None] & (boundary == 1)[:, None, None]
    return spread + jnp.where(opening, math.log(0.5), 0.0).astype(spread.dtype)


def projections(inputs, gain, heads):
    rows = inputs.shape[0]
    widened = inputs.astype(jnp.float32)
    result = []
    for index in range(3):
        rounded = lax.optimization_barrier((widened * gain[index]).astype(jnp.bfloat16))
        result.append(rounded.reshape(rows, heads, -1))
    return result


def local(inputs, out_grad, gains, exponent, boundary):
    block = inputs[0]
    grad_block = out_grad[0]
    gain = gains[0]
    rows, width = block.shape
    heads = exponent.shape[2]
    head_dim = width // heads
    scale = 1.0 / head_dim
    query_half, key_half, value_half = projections(block, gain, heads)
    grad_half = grad_block.reshape(rows, heads, head_dim)
    queries = query_half.astype(jnp.float32)
    key_rows = key_half.astype(jnp.float32)
    value_rows = value_half.astype(jnp.float32)
    grad_rows = grad_half.astype(jnp.float32)
    logs = decay_logs(exponent[0], boundary[0], CH).reshape(rows, heads)
    cumul = jnp.cumsum(logs, axis=0)
    growth = jnp.exp(cumul)
    tail = jnp.exp(cumul[-1][None, :] - cumul)
    forward_part = jnp.einsum(
        "shd,she->hde", key_rows * tail[:, :, None], value_rows, precision=HIGH
    )
    adjoint_part = scale * jnp.einsum(
        "shd,she->hde", queries * growth[:, :, None], grad_rows, precision=HIGH
    )
    whole_decay = jnp.exp(cumul[-1])
    cum_heads = cumul.T
    gap = cum_heads[:, :, None] - cum_heads[:, None, :]
    lower = jnp.arange(rows)[:, None] >= jnp.arange(rows)[None, :]
    decay = jnp.where(lower[None], jnp.exp(jnp.minimum(gap, 0.0)), 0.0)
    mixing = (
        jnp.einsum("thd,shd->hts", grad_half, value_half, preferred_element_type=jnp.float32)
        * decay
    )
    query_near = scale * jnp.einsum("hts,shd->thd", mixing, key_rows, precision=HIGH)
    key_near = scale * jnp.einsum("hts,thd->shd", mixing, queries, precision=HIGH)
    attention = (
        jnp.einsum("thd,shd->hts", query_half, key_half, preferred_element_type=jnp.float32) * decay
    )
    value_near = scale * jnp.einsum("hts,the->she", attention, grad_rows, precision=HIGH)
    near_total = grad_block.astype(jnp.float32)
    near_total = near_total + gain[0] * query_near.reshape(rows, width)
    near_total = near_total + gain[1] * key_near.reshape(rows, width)
    near_total = near_total + gain[2] * value_near.reshape(rows, width)
    near_round = near_total.astype(jnp.bfloat16)
    near_received = passed_along(near_round, "section", -1)
    state_in, adjoint_in, near_received = scans_in(
        forward_part, adjoint_part, whole_decay, "ctx", near_received
    )
    query_far = (
        scale * growth[:, :, None] * jnp.einsum("the,hde->thd", grad_rows, state_in, precision=HIGH)
    )
    key_far = tail[:, :, None] * jnp.einsum("she,hde->shd", value_rows, adjoint_in, precision=HIGH)
    value_far = tail[:, :, None] * jnp.einsum("shd,hde->she", key_rows, adjoint_in, precision=HIGH)
    far_total = gain[0] * query_far.reshape(rows, width)
    far_total = far_total + gain[1] * key_far.reshape(rows, width)
    far_total = far_total + gain[2] * value_far.reshape(rows, width)
    far_round = far_total.astype(jnp.bfloat16)
    far_received = passed_along(far_round, "section", -1)
    received = (near_received.astype(jnp.float32) + far_received.astype(jnp.float32)).astype(
        jnp.bfloat16
    )
    return received[None]


def solution(mesh):
    in_specs = (
        P("section", "ctx", None),
        P("section", "ctx", None),
        P("section", None, None),
        P("section", "ctx", None),
        P("section", "ctx"),
    )
    out_specs = P("section", "ctx", None)
    return jax.shard_map(local, mesh=mesh, in_specs=in_specs, out_specs=out_specs, check_vma=False)
```

```python
import math

import jax
import jax.numpy as jnp
from jax import lax
from jax.sharding import PartitionSpec as P

CH = 64


HIGH = lax.Precision.HIGH


def packed(state, rate):
    tile = jnp.broadcast_to(rate[:, None, None], (state.shape[0], 8, state.shape[2]))
    return jnp.concatenate([state, tile], axis=1)


def unpacked(message):
    width = message.shape[1] - 8
    return message[:, :width], message[:, width, 0]


def narrow(message):
    state, rate = unpacked(message)
    high = rate.astype(jnp.bfloat16)
    low = (rate - high.astype(jnp.float32)).astype(jnp.bfloat16)
    rows = jnp.stack([high, low] + [jnp.zeros_like(high)] * 6, axis=1)
    tile = jnp.broadcast_to(rows[:, :, None], (state.shape[0], 8, state.shape[2]))
    return jnp.concatenate([state.astype(jnp.bfloat16), tile], axis=1)


def widen(message):
    width = message.shape[1] - 8
    rate = message[:, width, 0].astype(jnp.float32) + message[:, width + 1, 0].astype(jnp.float32)
    return packed(message[:, :width].astype(jnp.float32), rate)


def sent_narrow(message, axis, pairs):
    return widen(lax.ppermute(narrow(message), axis, pairs))


def merged(farther, nearer):
    far_state, far_rate = unpacked(farther)
    near_state, near_rate = unpacked(nearer)
    return packed(near_rate[:, None, None] * far_state + near_state, far_rate * near_rate)


def both_ways(count, moves):
    return list(moves) + [(count - 1 - source, count - 1 - target) for source, target in moves]


def scans_in(forward_part, backward_part, rate, axis, held):
    count = lax.axis_size(axis)
    if count == 1:
        return jnp.zeros_like(forward_part), jnp.zeros_like(backward_part), held
    assert count % 2 == 0
    odd = lax.axis_index(axis) % 2 == 1
    couples = count // 2
    swap = [(2 * p, 2 * p + 1) for p in range(couples)] + [(2 * p + 1, 2 * p) for p in range(couples)]
    mine = jnp.where(odd, forward_part, backward_part)
    sent = packed(jnp.where(odd, backward_part, forward_part), rate)
    lower, lower_rate = unpacked(lax.ppermute(sent, axis, swap))
    window = packed(rate[:, None, None] * lower + mine, rate * lower_rate)
    if couples <= 4:
        incoming = jnp.zeros_like(mine)
        weight = jnp.ones_like(rate)
        for step in range(1, couples):
            moves = [(2 * p + 1, 2 * (p + step) + 1) for p in range(couples - step)]
            got, got_rate = unpacked(sent_narrow(window, axis, both_ways(count, moves)))
            incoming = incoming + weight[:, None, None] * got
            weight = weight * got_rate
    else:
        covered = 1
        while 2 * covered < couples:
            moves = [(2 * p + 1, 2 * (p + covered) + 1) for p in range(couples - covered)]
            window = merged(sent_narrow(window, axis, both_ways(count, moves)), window)
            covered *= 2
        moves = [(2 * p + 1, 2 * p + 3) for p in range(couples - 1)]
        nearer = sent_narrow(window, axis, both_ways(count, moves))
        if 1 + covered < couples:
            moves = [(2 * p + 1, 2 * (p + 1 + covered) + 1) for p in range(couples - 1 - covered)]
            nearer = merged(sent_narrow(window, axis, both_ways(count, moves)), nearer)
        incoming = unpacked(nearer)[0]
    incoming, held = lax.optimization_barrier((incoming, held))
    other = lax.ppermute(incoming, axis, swap)
    own = lower_rate[:, None, None] * incoming + lower
    return jnp.where(odd, own, other), jnp.where(odd, other, own), held


def passed_along(value, axis, steps):
    count = lax.axis_size(axis)
    pairs = [(source, (source + steps) % count) for source in range(count)]
    return lax.ppermute(value, axis, pairs)


def decay_logs(exponent, boundary, length):
    count, heads = exponent.shape
    rate = jnp.log(1.0 - exponent.astype(jnp.float32) / 65536.0)
    spread = jnp.broadcast_to(rate[:, None, :], (count, length, heads))
    opening = (jnp.arange(length) == 0)[None, :, None] & (boundary == 1)[:, None, None]
    return spread + jnp.where(opening, math.log(0.5), 0.0).astype(spread.dtype)


def projections(inputs, gain, heads):
    rows = inputs.shape[0]
    widened = inputs.astype(jnp.float32)
    result = []
    for index in range(3):
        rounded = lax.optimization_barrier((widened * gain[index]).astype(jnp.bfloat16))
        result.append(rounded.reshape(rows, heads, -1))
    return result


def local(inputs, out_grad, gains, exponent, boundary):
    block = inputs[0]
    grad_block = out_grad[0]
    gain = gains[0]
    rows, width = block.shape
    heads = exponent.shape[2]
    head_dim = width // heads
    scale = 1.0 / head_dim
    query_half, key_half, value_half = projections(block, gain, heads)
    grad_half = grad_block.reshape(rows, heads, head_dim)
    queries = query_half.astype(jnp.float32)
    key_rows = key_half.astype(jnp.float32)
    value_rows = value_half.astype(jnp.float32)
    grad_rows = grad_half.astype(jnp.float32)
    logs = decay_logs(exponent[0], boundary[0], CH).reshape(rows, heads)
    cumul = jnp.cumsum(logs, axis=0)
    growth = jnp.exp(cumul)
    tail = jnp.exp(cumul[-1][None, :] - cumul)
    forward_part = jnp.einsum(
        "shd,she->hde", key_rows * tail[:, :, None], value_rows, precision=HIGH
    )
    adjoint_part = scale * jnp.einsum(
        "shd,she->hde", queries * growth[:, :, None], grad_rows, precision=HIGH
    )
    whole_decay = jnp.exp(cumul[-1])
    cum_heads = cumul.T
    gap = cum_heads[:, :, None] - cum_heads[:, None, :]
    lower = jnp.arange(rows)[:, None] >= jnp.arange(rows)[None, :]
    decay = jnp.where(lower[None], jnp.exp(jnp.minimum(gap, 0.0)), 0.0)
    mixing = (
        jnp.einsum("thd,shd->hts", grad_half, value_half, preferred_element_type=jnp.float32)
        * decay
    )
    query_near = scale * jnp.einsum("hts,shd->thd", mixing, key_rows, precision=HIGH)
    key_near = scale * jnp.einsum("hts,thd->shd", mixing, queries, precision=HIGH)
    attention = (
        jnp.einsum("thd,shd->hts", query_half, key_half, preferred_element_type=jnp.float32) * decay
    )
    value_near = scale * jnp.einsum("hts,the->she", attention, grad_rows, precision=HIGH)
    near_total = grad_block.astype(jnp.float32)
    near_total = near_total + gain[0] * query_near.reshape(rows, width)
    near_total = near_total + gain[1] * key_near.reshape(rows, width)
    near_total = near_total + gain[2] * value_near.reshape(rows, width)
    near_round = near_total.astype(jnp.bfloat16)
    near_received = passed_along(near_round, "section", -1)
    state_in, adjoint_in, near_received = scans_in(
        forward_part, adjoint_part, whole_decay, "ctx", near_received
    )
    query_far = (
        scale * growth[:, :, None] * jnp.einsum("the,hde->thd", grad_rows, state_in, precision=HIGH)
    )
    key_far = tail[:, :, None] * jnp.einsum("she,hde->shd", value_rows, adjoint_in, precision=HIGH)
    value_far = tail[:, :, None] * jnp.einsum("shd,hde->she", key_rows, adjoint_in, precision=HIGH)
    far_total = gain[0] * query_far.reshape(rows, width)
    far_total = far_total + gain[1] * key_far.reshape(rows, width)
    far_total = far_total + gain[2] * value_far.reshape(rows, width)
    far_round = far_total.astype(jnp.bfloat16)
    far_received = passed_along(far_round, "section", -1)
    received = (near_received.astype(jnp.float32) + far_received.astype(jnp.float32)).astype(
        jnp.bfloat16
    )
    return received[None]


def solution(mesh):
    in_specs = (
        P("section", "ctx", None),
        P("section", "ctx", None),
        P("section", None, None),
        P("section", "ctx", None),
        P("section", "ctx"),
    )
    out_specs = P("section", "ctx", None)
    return jax.shard_map(local, mesh=mesh, in_specs=in_specs, out_specs=out_specs, check_vma=False)
```

```python
import math

import jax
import jax.numpy as jnp
from jax import lax
from jax.sharding import PartitionSpec as P

CH = 64


HIGH = lax.Precision.HIGH


def packed(state, rate):
    tile = jnp.broadcast_to(rate[:, None, None], (state.shape[0], 8, state.shape[2]))
    return jnp.concatenate([state, tile], axis=1)


def unpacked(message):
    width = message.shape[1] - 8
    return message[:, :width], message[:, width, 0]


def narrow(message):
    state, rate = unpacked(message)
    high = rate.astype(jnp.bfloat16)
    low = (rate - high.astype(jnp.float32)).astype(jnp.bfloat16)
    rows = jnp.stack([high, low] + [jnp.zeros_like(high)] * 6, axis=1)
    tile = jnp.broadcast_to(rows[:, :, None], (state.shape[0], 8, state.shape[2]))
    return jnp.concatenate([state.astype(jnp.bfloat16), tile], axis=1)


def widen(message):
    width = message.shape[1] - 8
    rate = message[:, width, 0].astype(jnp.float32) + message[:, width + 1, 0].astype(jnp.float32)
    return packed(message[:, :width].astype(jnp.float32), rate)


def sent_narrow(message, axis, pairs):
    return widen(lax.ppermute(narrow(message), axis, pairs))


def merged(farther, nearer):
    far_state, far_rate = unpacked(farther)
    near_state, near_rate = unpacked(nearer)
    return packed(near_rate[:, None, None] * far_state + near_state, far_rate * near_rate)


def both_ways(count, moves):
    return list(moves) + [(count - 1 - source, count - 1 - target) for source, target in moves]


def scans_in(forward_part, backward_part, rate, axis, held):
    count = lax.axis_size(axis)
    if count == 1:
        return jnp.zeros_like(forward_part), jnp.zeros_like(backward_part), held
    assert count % 2 == 0
    odd = lax.axis_index(axis) % 2 == 1
    couples = count // 2
    swap = [(2 * p, 2 * p + 1) for p in range(couples)] + [(2 * p + 1, 2 * p) for p in range(couples)]
    mine = jnp.where(odd, forward_part, backward_part)
    sent = packed(jnp.where(odd, backward_part, forward_part), rate)
    message = lax.ppermute(sent, axis, swap)
    lower, lower_rate = unpacked(message)
    window = rate[:, None, None] * message + packed(mine, jnp.zeros_like(rate))
    if couples <= 4:
        incoming = jnp.zeros_like(mine)
        weight = jnp.ones_like(rate)
        for step in range(1, couples):
            moves = [(2 * p + 1, 2 * (p + step) + 1) for p in range(couples - step)]
            got, got_rate = unpacked(sent_narrow(window, axis, both_ways(count, moves)))
            incoming = incoming + weight[:, None, None] * got
            weight = weight * got_rate
    else:
        covered = 1
        while 2 * covered < couples:
            moves = [(2 * p + 1, 2 * (p + covered) + 1) for p in range(couples - covered)]
            window = merged(sent_narrow(window, axis, both_ways(count, moves)), window)
            covered *= 2
        moves = [(2 * p + 1, 2 * p + 3) for p in range(couples - 1)]
        nearer = sent_narrow(window, axis, both_ways(count, moves))
        if 1 + covered < couples:
            moves = [(2 * p + 1, 2 * (p + 1 + covered) + 1) for p in range(couples - 1 - covered)]
            nearer = merged(sent_narrow(window, axis, both_ways(count, moves)), nearer)
        incoming = unpacked(nearer)[0]
    incoming, held = lax.optimization_barrier((incoming, held))
    other = lax.ppermute(incoming, axis, swap)
    own = lower_rate[:, None, None] * incoming + lower
    return jnp.where(odd, own, other), jnp.where(odd, other, own), held


def passed_along(value, axis, steps):
    count = lax.axis_size(axis)
    pairs = [(source, (source + steps) % count) for source in range(count)]
    return lax.ppermute(value, axis, pairs)


def decay_logs(exponent, boundary, length):
    count, heads = exponent.shape
    rate = jnp.log(1.0 - exponent.astype(jnp.float32) / 65536.0)
    spread = jnp.broadcast_to(rate[:, None, :], (count, length, heads))
    opening = (jnp.arange(length) == 0)[None, :, None] & (boundary == 1)[:, None, None]
    return spread + jnp.where(opening, math.log(0.5), 0.0).astype(spread.dtype)


def projections(inputs, gain, heads):
    rows = inputs.shape[0]
    widened = inputs.astype(jnp.float32)
    result = []
    for index in range(3):
        rounded = lax.optimization_barrier((widened * gain[index]).astype(jnp.bfloat16))
        result.append(rounded.reshape(rows, heads, -1))
    return result


def local(inputs, out_grad, gains, exponent, boundary):
    block = inputs[0]
    grad_block = out_grad[0]
    gain = gains[0]
    rows, width = block.shape
    heads = exponent.shape[2]
    head_dim = width // heads
    scale = 1.0 / head_dim
    query_half, key_half, value_half = projections(block, gain, heads)
    grad_half = grad_block.reshape(rows, heads, head_dim)
    queries = query_half.astype(jnp.float32)
    key_rows = key_half.astype(jnp.float32)
    value_rows = value_half.astype(jnp.float32)
    grad_rows = grad_half.astype(jnp.float32)
    logs = decay_logs(exponent[0], boundary[0], CH).reshape(rows, heads)
    cumul = jnp.cumsum(logs, axis=0)
    growth = jnp.exp(cumul)
    tail = jnp.exp(cumul[-1][None, :] - cumul)
    forward_part = jnp.einsum(
        "shd,she->hde", key_rows * tail[:, :, None], value_rows, precision=HIGH
    )
    adjoint_part = scale * jnp.einsum(
        "shd,she->hde", queries * growth[:, :, None], grad_rows, precision=HIGH
    )
    whole_decay = jnp.exp(cumul[-1])
    cum_heads = cumul.T
    gap = cum_heads[:, :, None] - cum_heads[:, None, :]
    lower = jnp.arange(rows)[:, None] >= jnp.arange(rows)[None, :]
    decay = jnp.where(lower[None], jnp.exp(jnp.minimum(gap, 0.0)), 0.0)
    mixing = (
        jnp.einsum("thd,shd->hts", grad_half, value_half, preferred_element_type=jnp.float32)
        * decay
    )
    query_near = scale * jnp.einsum("hts,shd->thd", mixing, key_rows, precision=HIGH)
    key_near = scale * jnp.einsum("hts,thd->shd", mixing, queries, precision=HIGH)
    attention = (
        jnp.einsum("thd,shd->hts", query_half, key_half, preferred_element_type=jnp.float32) * decay
    )
    value_near = scale * jnp.einsum("hts,the->she", attention, grad_rows, precision=HIGH)
    near_total = grad_block.astype(jnp.float32)
    near_total = near_total + gain[0] * query_near.reshape(rows, width)
    near_total = near_total + gain[1] * key_near.reshape(rows, width)
    near_total = near_total + gain[2] * value_near.reshape(rows, width)
    near_round = near_total.astype(jnp.bfloat16)
    near_received = passed_along(near_round, "section", -1)
    state_in, adjoint_in, near_received = scans_in(
        forward_part, adjoint_part, whole_decay, "ctx", near_received
    )
    query_far = (
        scale * growth[:, :, None] * jnp.einsum("the,hde->thd", grad_rows, state_in, precision=HIGH)
    )
    key_far = tail[:, :, None] * jnp.einsum("she,hde->shd", value_rows, adjoint_in, precision=HIGH)
    value_far = tail[:, :, None] * jnp.einsum("shd,hde->she", key_rows, adjoint_in, precision=HIGH)
    far_total = gain[0] * query_far.reshape(rows, width)
    far_total = far_total + gain[1] * key_far.reshape(rows, width)
    far_total = far_total + gain[2] * value_far.reshape(rows, width)
    far_round = far_total.astype(jnp.bfloat16)
    far_received = passed_along(far_round, "section", -1)
    received = (near_received.astype(jnp.float32) + far_received.astype(jnp.float32)).astype(
        jnp.bfloat16
    )
    return received[None]


def solution(mesh):
    in_specs = (
        P("section", "ctx", None),
        P("section", "ctx", None),
        P("section", None, None),
        P("section", "ctx", None),
        P("section", "ctx"),
    )
    out_specs = P("section", "ctx", None)
    return jax.shard_map(local, mesh=mesh, in_specs=in_specs, out_specs=out_specs, check_vma=False)
```

```python
import math

import jax
import jax.numpy as jnp
from jax import lax
from jax.sharding import PartitionSpec as P

CH = 64


HIGH = lax.Precision.HIGH


def packed(state, rate):
    tile = jnp.broadcast_to(rate[:, None, None], (state.shape[0], 8, state.shape[2]))
    return jnp.concatenate([state, tile], axis=1)


def unpacked(message):
    width = message.shape[1] - 8
    return message[:, :width], message[:, width, 0]


def narrow(message):
    state, rate = unpacked(message)
    high = rate.astype(jnp.bfloat16)
    low = (rate - high.astype(jnp.float32)).astype(jnp.bfloat16)
    rows = jnp.stack([high, low] + [jnp.zeros_like(high)] * 6, axis=1)
    tile = jnp.broadcast_to(rows[:, :, None], (state.shape[0], 8, state.shape[2]))
    return jnp.concatenate([state.astype(jnp.bfloat16), tile], axis=1)


def widen(message):
    width = message.shape[1] - 8
    rate = message[:, width, 0].astype(jnp.float32) + message[:, width + 1, 0].astype(jnp.float32)
    return packed(message[:, :width].astype(jnp.float32), rate)


def sent_narrow(message, axis, pairs):
    return widen(lax.ppermute(narrow(message), axis, pairs))


def merged(farther, nearer):
    far_state, far_rate = unpacked(farther)
    near_state, near_rate = unpacked(nearer)
    return packed(near_rate[:, None, None] * far_state + near_state, far_rate * near_rate)


def both_ways(count, moves):
    return list(moves) + [(count - 1 - source, count - 1 - target) for source, target in moves]


def scans_in(forward_part, backward_part, rate, axis, held):
    count = lax.axis_size(axis)
    if count == 1:
        return jnp.zeros_like(forward_part), jnp.zeros_like(backward_part), held
    assert count % 2 == 0
    odd = lax.axis_index(axis) % 2 == 1
    couples = count // 2
    swap = [(2 * p, 2 * p + 1) for p in range(couples)] + [(2 * p + 1, 2 * p) for p in range(couples)]
    mine = jnp.where(odd, forward_part, backward_part)
    sent = packed(jnp.where(odd, backward_part, forward_part), rate)
    message = lax.ppermute(sent, axis, swap)
    lower_rate = unpacked(message)[1]
    window = rate[:, None, None] * message + packed(mine, jnp.zeros_like(rate))
    if couples <= 4:
        incoming = jnp.zeros_like(window)
        weight = jnp.ones_like(rate)
        for step in range(1, couples):
            moves = [(2 * p + 1, 2 * (p + step) + 1) for p in range(couples - step)]
            got = sent_narrow(window, axis, both_ways(count, moves))
            incoming = incoming + weight[:, None, None] * got
            weight = weight * unpacked(got)[1]
    else:
        covered = 1
        while 2 * covered < couples:
            moves = [(2 * p + 1, 2 * (p + covered) + 1) for p in range(couples - covered)]
            window = merged(sent_narrow(window, axis, both_ways(count, moves)), window)
            covered *= 2
        moves = [(2 * p + 1, 2 * p + 3) for p in range(couples - 1)]
        nearer = sent_narrow(window, axis, both_ways(count, moves))
        if 1 + covered < couples:
            moves = [(2 * p + 1, 2 * (p + 1 + covered) + 1) for p in range(couples - 1 - covered)]
            nearer = merged(sent_narrow(window, axis, both_ways(count, moves)), nearer)
        incoming = nearer
    incoming, held = lax.optimization_barrier((incoming, held))
    other = lax.ppermute(incoming, axis, swap)
    own = lower_rate[:, None, None] * incoming + message
    width = message.shape[1] - 8
    forward_in = jnp.where(odd, own, other)[:, :width]
    backward_in = jnp.where(odd, other, own)[:, :width]
    return forward_in, backward_in, held


def passed_along(value, axis, steps):
    count = lax.axis_size(axis)
    pairs = [(source, (source + steps) % count) for source in range(count)]
    return lax.ppermute(value, axis, pairs)


def decay_logs(exponent, boundary, length):
    count, heads = exponent.shape
    rate = jnp.log(1.0 - exponent.astype(jnp.float32) / 65536.0)
    spread = jnp.broadcast_to(rate[:, None, :], (count, length, heads))
    opening = (jnp.arange(length) == 0)[None, :, None] & (boundary == 1)[:, None, None]
    return spread + jnp.where(opening, math.log(0.5), 0.0).astype(spread.dtype)


def projections(inputs, gain, heads):
    rows = inputs.shape[0]
    widened = inputs.astype(jnp.float32)
    result = []
    for index in range(3):
        rounded = lax.optimization_barrier((widened * gain[index]).astype(jnp.bfloat16))
        result.append(rounded.reshape(rows, heads, -1))
    return result


def local(inputs, out_grad, gains, exponent, boundary):
    block = inputs[0]
    grad_block = out_grad[0]
    gain = gains[0]
    rows, width = block.shape
    heads = exponent.shape[2]
    head_dim = width // heads
    scale = 1.0 / head_dim
    query_half, key_half, value_half = projections(block, gain, heads)
    grad_half = grad_block.reshape(rows, heads, head_dim)
    queries = query_half.astype(jnp.float32)
    key_rows = key_half.astype(jnp.float32)
    value_rows = value_half.astype(jnp.float32)
    grad_rows = grad_half.astype(jnp.float32)
    logs = decay_logs(exponent[0], boundary[0], CH).reshape(rows, heads)
    cumul = jnp.cumsum(logs, axis=0)
    growth = jnp.exp(cumul)
    tail = jnp.exp(cumul[-1][None, :] - cumul)
    forward_part = jnp.einsum(
        "shd,she->hde", key_rows * tail[:, :, None], value_rows, precision=HIGH
    )
    adjoint_part = scale * jnp.einsum(
        "shd,she->hde", queries * growth[:, :, None], grad_rows, precision=HIGH
    )
    whole_decay = jnp.exp(cumul[-1])
    cum_heads = cumul.T
    gap = cum_heads[:, :, None] - cum_heads[:, None, :]
    lower = jnp.arange(rows)[:, None] >= jnp.arange(rows)[None, :]
    decay = jnp.where(lower[None], jnp.exp(jnp.minimum(gap, 0.0)), 0.0)
    mixing = (
        jnp.einsum("thd,shd->hts", grad_half, value_half, preferred_element_type=jnp.float32)
        * decay
    )
    query_near = scale * jnp.einsum("hts,shd->thd", mixing, key_rows, precision=HIGH)
    key_near = scale * jnp.einsum("hts,thd->shd", mixing, queries, precision=HIGH)
    attention = (
        jnp.einsum("thd,shd->hts", query_half, key_half, preferred_element_type=jnp.float32) * decay
    )
    value_near = scale * jnp.einsum("hts,the->she", attention, grad_rows, precision=HIGH)
    near_total = grad_block.astype(jnp.float32)
    near_total = near_total + gain[0] * query_near.reshape(rows, width)
    near_total = near_total + gain[1] * key_near.reshape(rows, width)
    near_total = near_total + gain[2] * value_near.reshape(rows, width)
    near_round = near_total.astype(jnp.bfloat16)
    near_received = passed_along(near_round, "section", -1)
    state_in, adjoint_in, near_received = scans_in(
        forward_part, adjoint_part, whole_decay, "ctx", near_received
    )
    query_far = (
        scale * growth[:, :, None] * jnp.einsum("the,hde->thd", grad_rows, state_in, precision=HIGH)
    )
    key_far = tail[:, :, None] * jnp.einsum("she,hde->shd", value_rows, adjoint_in, precision=HIGH)
    value_far = tail[:, :, None] * jnp.einsum("shd,hde->she", key_rows, adjoint_in, precision=HIGH)
    far_total = gain[0] * query_far.reshape(rows, width)
    far_total = far_total + gain[1] * key_far.reshape(rows, width)
    far_total = far_total + gain[2] * value_far.reshape(rows, width)
    far_round = far_total.astype(jnp.bfloat16)
    far_received = passed_along(far_round, "section", -1)
    received = (near_received.astype(jnp.float32) + far_received.astype(jnp.float32)).astype(
        jnp.bfloat16
    )
    return received[None]


def solution(mesh):
    in_specs = (
        P("section", "ctx", None),
        P("section", "ctx", None),
        P("section", None, None),
        P("section", "ctx", None),
        P("section", "ctx"),
    )
    out_specs = P("section", "ctx", None)
    return jax.shard_map(local, mesh=mesh, in_specs=in_specs, out_specs=out_specs, check_vma=False)
```

```python
import math

import jax
import jax.numpy as jnp
from jax import lax
from jax.sharding import PartitionSpec as P

CH = 64


HIGH = lax.Precision.HIGH


def packed(state, rate):
    tile = jnp.broadcast_to(rate[:, None, None], (state.shape[0], 8, state.shape[2]))
    return jnp.concatenate([state, tile], axis=1)


def unpacked(message):
    width = message.shape[1] - 8
    return message[:, :width], message[:, width, 0]


def narrow(message):
    state, rate = unpacked(message)
    high = rate.astype(jnp.bfloat16)
    low = (rate - high.astype(jnp.float32)).astype(jnp.bfloat16)
    rows = jnp.stack([high, low] + [jnp.zeros_like(high)] * 6, axis=1)
    tile = jnp.broadcast_to(rows[:, :, None], (state.shape[0], 8, state.shape[2]))
    return jnp.concatenate([state.astype(jnp.bfloat16), tile], axis=1)


def widen(message):
    width = message.shape[1] - 8
    rate = message[:, width, 0].astype(jnp.float32) + message[:, width + 1, 0].astype(jnp.float32)
    return packed(message[:, :width].astype(jnp.float32), rate)


def sent_narrow(message, axis, pairs):
    return widen(lax.ppermute(narrow(message), axis, pairs))


def merged(farther, nearer):
    far_state, far_rate = unpacked(farther)
    near_state, near_rate = unpacked(nearer)
    return packed(near_rate[:, None, None] * far_state + near_state, far_rate * near_rate)


def both_ways(count, moves):
    return list(moves) + [(count - 1 - source, count - 1 - target) for source, target in moves]


def scans_in(forward_part, backward_part, rate, axis, held):
    count = lax.axis_size(axis)
    if count == 1:
        return jnp.zeros_like(forward_part), jnp.zeros_like(backward_part), held
    assert count % 2 == 0
    odd = lax.axis_index(axis) % 2 == 1
    couples = count // 2
    swap = [(2 * p, 2 * p + 1) for p in range(couples)] + [(2 * p + 1, 2 * p) for p in range(couples)]
    mine = jnp.where(odd, forward_part, backward_part)
    sent = packed(jnp.where(odd, backward_part, forward_part), rate)
    message = lax.ppermute(sent, axis, swap)
    lower_rate = unpacked(message)[1]
    window = rate[:, None, None] * message + packed(mine, jnp.zeros_like(rate))
    if couples <= 4:
        incoming = jnp.zeros_like(mine)
        weight = jnp.ones_like(rate)
        for step in range(1, couples):
            moves = [(2 * p + 1, 2 * (p + step) + 1) for p in range(couples - step)]
            got, got_rate = unpacked(sent_narrow(window, axis, both_ways(count, moves)))
            incoming = incoming + weight[:, None, None] * got
            weight = weight * got_rate
    else:
        covered = 1
        while 2 * covered < couples:
            moves = [(2 * p + 1, 2 * (p + covered) + 1) for p in range(couples - covered)]
            window = merged(sent_narrow(window, axis, both_ways(count, moves)), window)
            covered *= 2
        moves = [(2 * p + 1, 2 * p + 3) for p in range(couples - 1)]
        nearer = sent_narrow(window, axis, both_ways(count, moves))
        if 1 + covered < couples:
            moves = [(2 * p + 1, 2 * (p + 1 + covered) + 1) for p in range(couples - 1 - covered)]
            nearer = merged(sent_narrow(window, axis, both_ways(count, moves)), nearer)
        incoming = unpacked(nearer)[0]
    incoming, held = lax.optimization_barrier((incoming, held))
    other = lax.ppermute(incoming, axis, swap)
    width = message.shape[1] - 8
    own = (lower_rate[:, None, None] * packed(incoming, jnp.zeros_like(rate)) + message)[:, :width]
    return jnp.where(odd, own, other), jnp.where(odd, other, own), held


def passed_along(value, axis, steps):
    count = lax.axis_size(axis)
    pairs = [(source, (source + steps) % count) for source in range(count)]
    return lax.ppermute(value, axis, pairs)


def decay_logs(exponent, boundary, length):
    count, heads = exponent.shape
    rate = jnp.log(1.0 - exponent.astype(jnp.float32) / 65536.0)
    spread = jnp.broadcast_to(rate[:, None, :], (count, length, heads))
    opening = (jnp.arange(length) == 0)[None, :, None] & (boundary == 1)[:, None, None]
    return spread + jnp.where(opening, math.log(0.5), 0.0).astype(spread.dtype)


def projections(inputs, gain, heads):
    rows = inputs.shape[0]
    widened = inputs.astype(jnp.float32)
    result = []
    for index in range(3):
        rounded = lax.optimization_barrier((widened * gain[index]).astype(jnp.bfloat16))
        result.append(rounded.reshape(rows, heads, -1))
    return result


def local(inputs, out_grad, gains, exponent, boundary):
    block = inputs[0]
    grad_block = out_grad[0]
    gain = gains[0]
    rows, width = block.shape
    heads = exponent.shape[2]
    head_dim = width // heads
    scale = 1.0 / head_dim
    query_half, key_half, value_half = projections(block, gain, heads)
    grad_half = grad_block.reshape(rows, heads, head_dim)
    queries = query_half.astype(jnp.float32)
    key_rows = key_half.astype(jnp.float32)
    value_rows = value_half.astype(jnp.float32)
    grad_rows = grad_half.astype(jnp.float32)
    logs = decay_logs(exponent[0], boundary[0], CH).reshape(rows, heads)
    cumul = jnp.cumsum(logs, axis=0)
    growth = jnp.exp(cumul)
    tail = jnp.exp(cumul[-1][None, :] - cumul)
    forward_part = jnp.einsum(
        "shd,she->hde", key_rows * tail[:, :, None], value_rows, precision=HIGH
    )
    adjoint_part = scale * jnp.einsum(
        "shd,she->hde", queries * growth[:, :, None], grad_rows, precision=HIGH
    )
    whole_decay = jnp.exp(cumul[-1])
    cum_heads = cumul.T
    gap = cum_heads[:, :, None] - cum_heads[:, None, :]
    lower = jnp.arange(rows)[:, None] >= jnp.arange(rows)[None, :]
    decay = jnp.where(lower[None], jnp.exp(jnp.minimum(gap, 0.0)), 0.0)
    mixing = (
        jnp.einsum("thd,shd->hts", grad_half, value_half, preferred_element_type=jnp.float32)
        * decay
    )
    query_near = scale * jnp.einsum("hts,shd->thd", mixing, key_rows, precision=HIGH)
    key_near = scale * jnp.einsum("hts,thd->shd", mixing, queries, precision=HIGH)
    attention = (
        jnp.einsum("thd,shd->hts", query_half, key_half, preferred_element_type=jnp.float32) * decay
    )
    value_near = scale * jnp.einsum("hts,the->she", attention, grad_rows, precision=HIGH)
    near_total = grad_block.astype(jnp.float32)
    near_total = near_total + gain[0] * query_near.reshape(rows, width)
    near_total = near_total + gain[1] * key_near.reshape(rows, width)
    near_total = near_total + gain[2] * value_near.reshape(rows, width)
    near_round = near_total.astype(jnp.bfloat16)
    near_received = passed_along(near_round, "section", -1)
    state_in, adjoint_in, near_received = scans_in(
        forward_part, adjoint_part, whole_decay, "ctx", near_received
    )
    query_far = (
        scale * growth[:, :, None] * jnp.einsum("the,hde->thd", grad_rows, state_in, precision=HIGH)
    )
    key_far = tail[:, :, None] * jnp.einsum("she,hde->shd", value_rows, adjoint_in, precision=HIGH)
    value_far = tail[:, :, None] * jnp.einsum("shd,hde->she", key_rows, adjoint_in, precision=HIGH)
    far_total = gain[0] * query_far.reshape(rows, width)
    far_total = far_total + gain[1] * key_far.reshape(rows, width)
    far_total = far_total + gain[2] * value_far.reshape(rows, width)
    far_round = far_total.astype(jnp.bfloat16)
    far_received = passed_along(far_round, "section", -1)
    received = (near_received.astype(jnp.float32) + far_received.astype(jnp.float32)).astype(
        jnp.bfloat16
    )
    return received[None]


def solution(mesh):
    in_specs = (
        P("section", "ctx", None),
        P("section", "ctx", None),
        P("section", None, None),
        P("section", "ctx", None),
        P("section", "ctx"),
    )
    out_specs = P("section", "ctx", None)
    return jax.shard_map(local, mesh=mesh, in_specs=in_specs, out_specs=out_specs, check_vma=False)
```

```python
import math

import jax
import jax.numpy as jnp
from jax import lax
from jax.sharding import PartitionSpec as P

CH = 64


HIGH = lax.Precision.HIGH


def packed(state, rate):
    tile = jnp.broadcast_to(rate[:, None, None], (state.shape[0], 8, state.shape[2]))
    return jnp.concatenate([state, tile], axis=1)


def unpacked(message):
    width = message.shape[1] - 8
    return message[:, :width], message[:, width, 0]


def narrow(message):
    state, rate = unpacked(message)
    high = rate.astype(jnp.bfloat16)
    low = (rate - high.astype(jnp.float32)).astype(jnp.bfloat16)
    rows = jnp.stack([high, low] + [jnp.zeros_like(high)] * 6, axis=1)
    tile = jnp.broadcast_to(rows[:, :, None], (state.shape[0], 8, state.shape[2]))
    return jnp.concatenate([state.astype(jnp.bfloat16), tile], axis=1)


def widen(message):
    width = message.shape[1] - 8
    rate = message[:, width, 0].astype(jnp.float32) + message[:, width + 1, 0].astype(jnp.float32)
    return packed(message[:, :width].astype(jnp.float32), rate)


def sent_narrow(message, axis, pairs):
    return widen(lax.ppermute(narrow(message), axis, pairs))


def merged(farther, nearer):
    far_state, far_rate = unpacked(farther)
    near_state, near_rate = unpacked(nearer)
    return packed(near_rate[:, None, None] * far_state + near_state, far_rate * near_rate)


def both_ways(count, moves):
    return list(moves) + [(count - 1 - source, count - 1 - target) for source, target in moves]


def scans_in(forward_part, backward_part, rate, axis, held):
    count = lax.axis_size(axis)
    if count == 1:
        return jnp.zeros_like(forward_part[:, :-8]), jnp.zeros_like(backward_part[:, :-8]), held
    assert count % 2 == 0
    odd = lax.axis_index(axis) % 2 == 1
    couples = count // 2
    swap = [(2 * p, 2 * p + 1) for p in range(couples)] + [(2 * p + 1, 2 * p) for p in range(couples)]
    width = forward_part.shape[1] - 8
    tile = packed(jnp.zeros_like(forward_part[:, :width]), rate)
    sent = jnp.where(odd, backward_part, forward_part) + tile
    message = lax.ppermute(sent, axis, swap)
    lower, lower_rate = unpacked(message)
    window = rate[:, None, None] * message + jnp.where(odd, forward_part, backward_part)
    if couples <= 4:
        incoming = jnp.zeros_like(lower)
        weight = jnp.ones_like(rate)
        for step in range(1, couples):
            moves = [(2 * p + 1, 2 * (p + step) + 1) for p in range(couples - step)]
            got, got_rate = unpacked(sent_narrow(window, axis, both_ways(count, moves)))
            incoming = incoming + weight[:, None, None] * got
            weight = weight * got_rate
    else:
        covered = 1
        while 2 * covered < couples:
            moves = [(2 * p + 1, 2 * (p + covered) + 1) for p in range(couples - covered)]
            window = merged(sent_narrow(window, axis, both_ways(count, moves)), window)
            covered *= 2
        moves = [(2 * p + 1, 2 * p + 3) for p in range(couples - 1)]
        nearer = sent_narrow(window, axis, both_ways(count, moves))
        if 1 + covered < couples:
            moves = [(2 * p + 1, 2 * (p + 1 + covered) + 1) for p in range(couples - 1 - covered)]
            nearer = merged(sent_narrow(window, axis, both_ways(count, moves)), nearer)
        incoming = unpacked(nearer)[0]
    incoming, held = lax.optimization_barrier((incoming, held))
    other = lax.ppermute(incoming, axis, swap)
    own = lower_rate[:, None, None] * incoming + lower
    return jnp.where(odd, own, other), jnp.where(odd, other, own), held


def passed_along(value, axis, steps):
    count = lax.axis_size(axis)
    pairs = [(source, (source + steps) % count) for source in range(count)]
    return lax.ppermute(value, axis, pairs)


def decay_logs(exponent, boundary, length):
    count, heads = exponent.shape
    rate = jnp.log(1.0 - exponent.astype(jnp.float32) / 65536.0)
    spread = jnp.broadcast_to(rate[:, None, :], (count, length, heads))
    opening = (jnp.arange(length) == 0)[None, :, None] & (boundary == 1)[:, None, None]
    return spread + jnp.where(opening, math.log(0.5), 0.0).astype(spread.dtype)


def projections(inputs, gain, heads):
    rows = inputs.shape[0]
    widened = inputs.astype(jnp.float32)
    result = []
    for index in range(3):
        rounded = lax.optimization_barrier((widened * gain[index]).astype(jnp.bfloat16))
        result.append(rounded.reshape(rows, heads, -1))
    return result


def local(inputs, out_grad, gains, exponent, boundary):
    block = inputs[0]
    grad_block = out_grad[0]
    gain = gains[0]
    rows, width = block.shape
    heads = exponent.shape[2]
    head_dim = width // heads
    scale = 1.0 / head_dim
    query_half, key_half, value_half = projections(block, gain, heads)
    grad_half = grad_block.reshape(rows, heads, head_dim)
    queries = query_half.astype(jnp.float32)
    key_rows = key_half.astype(jnp.float32)
    value_rows = value_half.astype(jnp.float32)
    grad_rows = grad_half.astype(jnp.float32)
    logs = decay_logs(exponent[0], boundary[0], CH).reshape(rows, heads)
    cumul = jnp.cumsum(logs, axis=0)
    growth = jnp.exp(cumul)
    tail = jnp.exp(cumul[-1][None, :] - cumul)
    widened = ((0, 0), (0, 0), (0, 8))
    forward_part = jnp.einsum(
        "shd,she->hde", jnp.pad(key_rows * tail[:, :, None], widened), value_rows, precision=HIGH
    )
    adjoint_part = scale * jnp.einsum(
        "shd,she->hde", jnp.pad(queries * growth[:, :, None], widened), grad_rows, precision=HIGH
    )
    whole_decay = jnp.exp(cumul[-1])
    cum_heads = cumul.T
    gap = cum_heads[:, :, None] - cum_heads[:, None, :]
    lower = jnp.arange(rows)[:, None] >= jnp.arange(rows)[None, :]
    decay = jnp.where(lower[None], jnp.exp(jnp.minimum(gap, 0.0)), 0.0)
    mixing = (
        jnp.einsum("thd,shd->hts", grad_half, value_half, preferred_element_type=jnp.float32)
        * decay
    )
    query_near = scale * jnp.einsum("hts,shd->thd", mixing, key_rows, precision=HIGH)
    key_near = scale * jnp.einsum("hts,thd->shd", mixing, queries, precision=HIGH)
    attention = (
        jnp.einsum("thd,shd->hts", query_half, key_half, preferred_element_type=jnp.float32) * decay
    )
    value_near = scale * jnp.einsum("hts,the->she", attention, grad_rows, precision=HIGH)
    near_total = grad_block.astype(jnp.float32)
    near_total = near_total + gain[0] * query_near.reshape(rows, width)
    near_total = near_total + gain[1] * key_near.reshape(rows, width)
    near_total = near_total + gain[2] * value_near.reshape(rows, width)
    near_round = near_total.astype(jnp.bfloat16)
    near_received = passed_along(near_round, "section", -1)
    state_in, adjoint_in, near_received = scans_in(
        forward_part, adjoint_part, whole_decay, "ctx", near_received
    )
    query_far = (
        scale * growth[:, :, None] * jnp.einsum("the,hde->thd", grad_rows, state_in, precision=HIGH)
    )
    key_far = tail[:, :, None] * jnp.einsum("she,hde->shd", value_rows, adjoint_in, precision=HIGH)
    value_far = tail[:, :, None] * jnp.einsum("shd,hde->she", key_rows, adjoint_in, precision=HIGH)
    far_total = gain[0] * query_far.reshape(rows, width)
    far_total = far_total + gain[1] * key_far.reshape(rows, width)
    far_total = far_total + gain[2] * value_far.reshape(rows, width)
    far_round = far_total.astype(jnp.bfloat16)
    far_received = passed_along(far_round, "section", -1)
    received = (near_received.astype(jnp.float32) + far_received.astype(jnp.float32)).astype(
        jnp.bfloat16
    )
    return received[None]


def solution(mesh):
    in_specs = (
        P("section", "ctx", None),
        P("section", "ctx", None),
        P("section", None, None),
        P("section", "ctx", None),
        P("section", "ctx"),
    )
    out_specs = P("section", "ctx", None)
    return jax.shard_map(local, mesh=mesh, in_specs=in_specs, out_specs=out_specs, check_vma=False)
```

```python
import math

import jax
import jax.numpy as jnp
from jax import lax
from jax.sharding import PartitionSpec as P

CH = 64


HIGH = lax.Precision.HIGH


def packed(state, rate):
    tile = jnp.broadcast_to(rate[:, None, None], (state.shape[0], 8, state.shape[2]))
    return jnp.concatenate([state, tile], axis=1)


def unpacked(message):
    width = message.shape[1] - 8
    return message[:, :width], message[:, width, 0]


def narrow(message):
    state, rate = unpacked(message)
    high = rate.astype(jnp.bfloat16)
    low = (rate - high.astype(jnp.float32)).astype(jnp.bfloat16)
    rows = jnp.stack([high, low] + [jnp.zeros_like(high)] * 6, axis=1)
    tile = jnp.broadcast_to(rows[:, :, None], (state.shape[0], 8, state.shape[2]))
    return jnp.concatenate([state.astype(jnp.bfloat16), tile], axis=1)


def widen(message):
    width = message.shape[1] - 8
    rate = message[:, width, 0].astype(jnp.float32) + message[:, width + 1, 0].astype(jnp.float32)
    return packed(message[:, :width].astype(jnp.float32), rate)


def sent_narrow(message, axis, pairs):
    return widen(lax.ppermute(narrow(message), axis, pairs))


def merged(farther, nearer):
    far_state, far_rate = unpacked(farther)
    near_state, near_rate = unpacked(nearer)
    return packed(near_rate[:, None, None] * far_state + near_state, far_rate * near_rate)


def both_ways(count, moves):
    return list(moves) + [(count - 1 - source, count - 1 - target) for source, target in moves]


def scans_in(forward_part, backward_part, rate, axis, held):
    count = lax.axis_size(axis)
    if count == 1:
        return jnp.zeros_like(forward_part), jnp.zeros_like(backward_part), held
    assert count % 2 == 0
    odd = lax.axis_index(axis) % 2 == 1
    couples = count // 2
    swap = [(2 * p, 2 * p + 1) for p in range(couples)] + [(2 * p + 1, 2 * p) for p in range(couples)]
    mine = jnp.where(odd, forward_part, backward_part)
    sent = packed(jnp.where(odd, backward_part, forward_part), rate)
    message = lax.ppermute(sent, axis, swap)
    lower, lower_rate = unpacked(message)
    window = rate[:, None, None] * message + packed(mine, jnp.zeros_like(rate))
    if couples <= 4:
        incoming = jnp.zeros_like(mine)
        weight = jnp.ones_like(rate)
        for step in range(1, couples):
            moves = [(2 * p + 1, 2 * (p + step) + 1) for p in range(couples - step)]
            if step == couples - 1:
                bare = unpacked(window)[0].astype(jnp.bfloat16)
                got = lax.ppermute(bare, axis, both_ways(count, moves)).astype(jnp.float32)
                incoming = incoming + weight[:, None, None] * got
                continue
            got, got_rate = unpacked(sent_narrow(window, axis, both_ways(count, moves)))
            incoming = incoming + weight[:, None, None] * got
            weight = weight * got_rate
    else:
        covered = 1
        while 2 * covered < couples:
            moves = [(2 * p + 1, 2 * (p + covered) + 1) for p in range(couples - covered)]
            window = merged(sent_narrow(window, axis, both_ways(count, moves)), window)
            covered *= 2
        moves = [(2 * p + 1, 2 * p + 3) for p in range(couples - 1)]
        nearer = sent_narrow(window, axis, both_ways(count, moves))
        if 1 + covered < couples:
            moves = [(2 * p + 1, 2 * (p + 1 + covered) + 1) for p in range(couples - 1 - covered)]
            nearer = merged(sent_narrow(window, axis, both_ways(count, moves)), nearer)
        incoming = unpacked(nearer)[0]
    incoming, held = lax.optimization_barrier((incoming, held))
    other = lax.ppermute(incoming, axis, swap)
    own = lower_rate[:, None, None] * incoming + lower
    return jnp.where(odd, own, other), jnp.where(odd, other, own), held


def passed_along(value, axis, steps):
    count = lax.axis_size(axis)
    pairs = [(source, (source + steps) % count) for source in range(count)]
    return lax.ppermute(value, axis, pairs)


def decay_logs(exponent, boundary, length):
    count, heads = exponent.shape
    rate = jnp.log(1.0 - exponent.astype(jnp.float32) / 65536.0)
    spread = jnp.broadcast_to(rate[:, None, :], (count, length, heads))
    opening = (jnp.arange(length) == 0)[None, :, None] & (boundary == 1)[:, None, None]
    return spread + jnp.where(opening, math.log(0.5), 0.0).astype(spread.dtype)


def projections(inputs, gain, heads):
    rows = inputs.shape[0]
    widened = inputs.astype(jnp.float32)
    result = []
    for index in range(3):
        rounded = lax.optimization_barrier((widened * gain[index]).astype(jnp.bfloat16))
        result.append(rounded.reshape(rows, heads, -1))
    return result


def local(inputs, out_grad, gains, exponent, boundary):
    block = inputs[0]
    grad_block = out_grad[0]
    gain = gains[0]
    rows, width = block.shape
    heads = exponent.shape[2]
    head_dim = width // heads
    scale = 1.0 / head_dim
    query_half, key_half, value_half = projections(block, gain, heads)
    grad_half = grad_block.reshape(rows, heads, head_dim)
    queries = query_half.astype(jnp.float32)
    key_rows = key_half.astype(jnp.float32)
    value_rows = value_half.astype(jnp.float32)
    grad_rows = grad_half.astype(jnp.float32)
    logs = decay_logs(exponent[0], boundary[0], CH).reshape(rows, heads)
    cumul = jnp.cumsum(logs, axis=0)
    growth = jnp.exp(cumul)
    tail = jnp.exp(cumul[-1][None, :] - cumul)
    forward_part = jnp.einsum(
        "shd,she->hde", key_rows * tail[:, :, None], value_rows, precision=HIGH
    )
    adjoint_part = scale * jnp.einsum(
        "shd,she->hde", queries * growth[:, :, None], grad_rows, precision=HIGH
    )
    whole_decay = jnp.exp(cumul[-1])
    cum_heads = cumul.T
    gap = cum_heads[:, :, None] - cum_heads[:, None, :]
    lower = jnp.arange(rows)[:, None] >= jnp.arange(rows)[None, :]
    decay = jnp.where(lower[None], jnp.exp(jnp.minimum(gap, 0.0)), 0.0)
    mixing = (
        jnp.einsum("thd,shd->hts", grad_half, value_half, preferred_element_type=jnp.float32)
        * decay
    )
    query_near = scale * jnp.einsum("hts,shd->thd", mixing, key_rows, precision=HIGH)
    key_near = scale * jnp.einsum("hts,thd->shd", mixing, queries, precision=HIGH)
    attention = (
        jnp.einsum("thd,shd->hts", query_half, key_half, preferred_element_type=jnp.float32) * decay
    )
    value_near = scale * jnp.einsum("hts,the->she", attention, grad_rows, precision=HIGH)
    near_total = grad_block.astype(jnp.float32)
    near_total = near_total + gain[0] * query_near.reshape(rows, width)
    near_total = near_total + gain[1] * key_near.reshape(rows, width)
    near_total = near_total + gain[2] * value_near.reshape(rows, width)
    near_round = near_total.astype(jnp.bfloat16)
    near_received = passed_along(near_round, "section", -1)
    state_in, adjoint_in, near_received = scans_in(
        forward_part, adjoint_part, whole_decay, "ctx", near_received
    )
    query_far = (
        scale * growth[:, :, None] * jnp.einsum("the,hde->thd", grad_rows, state_in, precision=HIGH)
    )
    key_far = tail[:, :, None] * jnp.einsum("she,hde->shd", value_rows, adjoint_in, precision=HIGH)
    value_far = tail[:, :, None] * jnp.einsum("shd,hde->she", key_rows, adjoint_in, precision=HIGH)
    far_total = gain[0] * query_far.reshape(rows, width)
    far_total = far_total + gain[1] * key_far.reshape(rows, width)
    far_total = far_total + gain[2] * value_far.reshape(rows, width)
    far_round = far_total.astype(jnp.bfloat16)
    far_received = passed_along(far_round, "section", -1)
    received = (near_received.astype(jnp.float32) + far_received.astype(jnp.float32)).astype(
        jnp.bfloat16
    )
    return received[None]


def solution(mesh):
    in_specs = (
        P("section", "ctx", None),
        P("section", "ctx", None),
        P("section", None, None),
        P("section", "ctx", None),
        P("section", "ctx"),
    )
    out_specs = P("section", "ctx", None)
    return jax.shard_map(local, mesh=mesh, in_specs=in_specs, out_specs=out_specs, check_vma=False)
```

```python
import math

import jax
import jax.numpy as jnp
from jax import lax
from jax.sharding import PartitionSpec as P

CH = 64


HIGH = lax.Precision.HIGH


def packed(state, rate):
    tile = jnp.broadcast_to(rate[:, None, None], (state.shape[0], 8, state.shape[2]))
    return jnp.concatenate([state, tile], axis=1)


def unpacked(message):
    width = message.shape[1] - 8
    return message[:, :width], message[:, width, 0]


def narrow(message):
    state, rate = unpacked(message)
    high = rate.astype(jnp.bfloat16)
    low = (rate - high.astype(jnp.float32)).astype(jnp.bfloat16)
    rows = jnp.stack([high, low] + [jnp.zeros_like(high)] * 6, axis=1)
    tile = jnp.broadcast_to(rows[:, :, None], (state.shape[0], 8, state.shape[2]))
    return jnp.concatenate([state.astype(jnp.bfloat16), tile], axis=1)


def widen(message):
    width = message.shape[1] - 8
    rate = message[:, width, 0].astype(jnp.float32) + message[:, width + 1, 0].astype(jnp.float32)
    return packed(message[:, :width].astype(jnp.float32), rate)


def sent_narrow(message, axis, pairs):
    return widen(lax.ppermute(narrow(message), axis, pairs))


def merged(farther, nearer):
    far_state, far_rate = unpacked(farther)
    near_state, near_rate = unpacked(nearer)
    return packed(near_rate[:, None, None] * far_state + near_state, far_rate * near_rate)


def both_ways(count, moves):
    return list(moves) + [(count - 1 - source, count - 1 - target) for source, target in moves]


def scans_in(forward_part, backward_part, rate, axis, held):
    count = lax.axis_size(axis)
    if count == 1:
        return jnp.zeros_like(forward_part), jnp.zeros_like(backward_part), held
    assert count % 2 == 0
    odd = lax.axis_index(axis) % 2 == 1
    couples = count // 2
    swap = [(2 * p, 2 * p + 1) for p in range(couples)] + [(2 * p + 1, 2 * p) for p in range(couples)]
    mine = jnp.where(odd, forward_part, backward_part)
    sent = packed(jnp.where(odd, backward_part, forward_part), rate)
    message = lax.ppermute(sent, axis, swap)
    lower, lower_rate = unpacked(message)
    window = rate[:, None, None] * message + packed(mine, jnp.zeros_like(rate))
    if couples <= 4:
        incoming = jnp.zeros_like(mine)
        weight = jnp.ones_like(rate)
        for step in range(1, couples):
            moves = [(2 * p + 1, 2 * (p + step) + 1) for p in range(couples - step)]
            got, got_rate = unpacked(sent_narrow(window, axis, both_ways(count, moves)))
            incoming = incoming + weight[:, None, None] * got
            weight = weight * got_rate
    else:
        covered = 1
        while 2 * covered < couples:
            moves = [(2 * p + 1, 2 * (p + covered) + 1) for p in range(couples - covered)]
            window = merged(sent_narrow(window, axis, both_ways(count, moves)), window)
            covered *= 2
        moves = [(2 * p + 1, 2 * p + 3) for p in range(couples - 1)]
        nearer = sent_narrow(window, axis, both_ways(count, moves))
        if 1 + covered < couples:
            moves = [(2 * p + 1, 2 * (p + 1 + covered) + 1) for p in range(couples - 1 - covered)]
            nearer = merged(sent_narrow(window, axis, both_ways(count, moves)), nearer)
        incoming = unpacked(nearer)[0]
    incoming, held = lax.optimization_barrier((incoming, held))
    other = lax.ppermute(incoming, axis, swap)
    own = lower_rate[:, None, None] * incoming + lower
    return jnp.where(odd, own, other), jnp.where(odd, other, own), held


def passed_along(value, axis, steps):
    count = lax.axis_size(axis)
    pairs = [(source, (source + steps) % count) for source in range(count)]
    return lax.ppermute(value, axis, pairs)


def decay_logs(exponent, boundary, length):
    count, heads = exponent.shape
    rate = jnp.log(1.0 - exponent.astype(jnp.float32) / 65536.0)
    spread = jnp.broadcast_to(rate[:, None, :], (count, length, heads))
    opening = (jnp.arange(length) == 0)[None, :, None] & (boundary == 1)[:, None, None]
    return spread + jnp.where(opening, math.log(0.5), 0.0).astype(spread.dtype)


def projections(inputs, gain, heads):
    rows = inputs.shape[0]
    widened = inputs.astype(jnp.float32)
    result = []
    for index in range(3):
        rounded = lax.optimization_barrier((widened * gain[index]).astype(jnp.bfloat16))
        result.append(rounded.reshape(rows, heads, -1))
    return result


def local(inputs, out_grad, gains, exponent, boundary):
    block = inputs[0]
    grad_block = out_grad[0]
    gain = gains[0]
    rows, width = block.shape
    heads = exponent.shape[2]
    head_dim = width // heads
    scale = 1.0 / head_dim
    query_half, key_half, value_half = projections(block, gain, heads)
    grad_half = grad_block.reshape(rows, heads, head_dim)
    queries = query_half.astype(jnp.float32)
    key_rows = key_half.astype(jnp.float32)
    value_rows = value_half.astype(jnp.float32)
    grad_rows = grad_half.astype(jnp.float32)
    logs = decay_logs(exponent[0], boundary[0], CH).reshape(rows, heads)
    cumul = jnp.cumsum(logs, axis=0)
    growth = jnp.exp(cumul)
    tail = jnp.exp(cumul[-1][None, :] - cumul)
    forward_part = jnp.einsum(
        "shd,she->hde", key_rows * tail[:, :, None], value_rows, precision=HIGH
    )
    adjoint_part = scale * jnp.einsum(
        "shd,she->hde", queries * growth[:, :, None], grad_rows, precision=HIGH
    )
    whole_decay = jnp.exp(cumul[-1])
    cum_heads = cumul.T
    gap = cum_heads[:, :, None] - cum_heads[:, None, :]
    lower = jnp.arange(rows)[:, None] >= jnp.arange(rows)[None, :]
    decay = jnp.where(lower[None], jnp.exp(jnp.minimum(gap, 0.0)), 0.0)
    mixing = (
        jnp.einsum("thd,shd->hts", grad_half, value_half, preferred_element_type=jnp.float32)
        * decay
    )
    query_near = scale * jnp.einsum("hts,shd->thd", mixing, key_rows, precision=HIGH)
    key_near = scale * jnp.einsum("hts,thd->shd", mixing, queries, precision=HIGH)
    attention = (
        jnp.einsum("thd,shd->hts", query_half, key_half, preferred_element_type=jnp.float32) * decay
    )
    value_near = scale * jnp.einsum("hts,the->she", attention, grad_rows, precision=HIGH)
    near_total = grad_block.astype(jnp.float32)
    near_total = near_total + gain[0] * query_near.reshape(rows, width)
    near_total = near_total + gain[1] * key_near.reshape(rows, width)
    near_total = near_total + gain[2] * value_near.reshape(rows, width)
    near_round = near_total.astype(jnp.bfloat16)
    near_received = near_round
    state_in, adjoint_in, near_received = scans_in(
        forward_part, adjoint_part, whole_decay, "ctx", near_received
    )
    query_far = (
        scale * growth[:, :, None] * jnp.einsum("the,hde->thd", grad_rows, state_in, precision=HIGH)
    )
    key_far = tail[:, :, None] * jnp.einsum("she,hde->shd", value_rows, adjoint_in, precision=HIGH)
    value_far = tail[:, :, None] * jnp.einsum("shd,hde->she", key_rows, adjoint_in, precision=HIGH)
    far_total = gain[0] * query_far.reshape(rows, width)
    far_total = far_total + gain[1] * key_far.reshape(rows, width)
    far_total = far_total + gain[2] * value_far.reshape(rows, width)
    far_round = far_total.astype(jnp.bfloat16)
    near_kept, far_kept = lax.optimization_barrier((near_received, far_round))
    outgoing = (near_kept.astype(jnp.float32) + far_kept.astype(jnp.float32)).astype(jnp.bfloat16)
    received = passed_along(outgoing, "section", -1)
    return received[None]


def solution(mesh):
    in_specs = (
        P("section", "ctx", None),
        P("section", "ctx", None),
        P("section", None, None),
        P("section", "ctx", None),
        P("section", "ctx"),
    )
    out_specs = P("section", "ctx", None)
    return jax.shard_map(local, mesh=mesh, in_specs=in_specs, out_specs=out_specs, check_vma=False)
```

```python
import math

import jax
import jax.numpy as jnp
from jax import lax
from jax.sharding import PartitionSpec as P

CH = 64


HIGH = lax.Precision.HIGH


def packed(state, rate):
    tile = jnp.broadcast_to(rate[:, None, None], (state.shape[0], 8, state.shape[2]))
    return jnp.concatenate([state, tile], axis=1)


def unpacked(message):
    width = message.shape[1] - 8
    return message[:, :width], message[:, width, 0]


def narrow(message):
    state, rate = unpacked(message)
    high = rate.astype(jnp.bfloat16)
    low = (rate - high.astype(jnp.float32)).astype(jnp.bfloat16)
    rows = jnp.stack([high, low] + [jnp.zeros_like(high)] * 6, axis=1)
    tile = jnp.broadcast_to(rows[:, :, None], (state.shape[0], 8, state.shape[2]))
    return jnp.concatenate([state.astype(jnp.bfloat16), tile], axis=1)


def widen(message):
    width = message.shape[1] - 8
    rate = message[:, width, 0].astype(jnp.float32) + message[:, width + 1, 0].astype(jnp.float32)
    return packed(message[:, :width].astype(jnp.float32), rate)


def sent_narrow(message, axis, pairs):
    return widen(lax.ppermute(narrow(message), axis, pairs))


def merged(farther, nearer):
    far_state, far_rate = unpacked(farther)
    near_state, near_rate = unpacked(nearer)
    return packed(near_rate[:, None, None] * far_state + near_state, far_rate * near_rate)


def both_ways(count, moves):
    return list(moves) + [(count - 1 - source, count - 1 - target) for source, target in moves]


def scans_in(forward_part, backward_part, rate, axis, held):
    count = lax.axis_size(axis)
    if count == 1:
        return jnp.zeros_like(forward_part), jnp.zeros_like(backward_part), held
    assert count % 2 == 0
    odd = lax.axis_index(axis) % 2 == 1
    couples = count // 2
    swap = [(2 * p, 2 * p + 1) for p in range(couples)] + [(2 * p + 1, 2 * p) for p in range(couples)]
    mine = jnp.where(odd, forward_part, backward_part)
    sent = packed(jnp.where(odd, backward_part, forward_part), rate)
    message = lax.ppermute(sent, axis, swap)
    lower, lower_rate = unpacked(message)
    window = rate[:, None, None] * message + packed(mine, jnp.zeros_like(rate))
    if couples <= 4:
        incoming = jnp.zeros_like(mine)
        weight = jnp.ones_like(rate)
        for step in range(1, couples):
            moves = [(2 * p + 1, 2 * (p + step) + 1) for p in range(couples - step)]
            got, got_rate = unpacked(sent_narrow(window, axis, both_ways(count, moves)))
            incoming = incoming + weight[:, None, None] * got
            weight = weight * got_rate
    else:
        covered = 1
        while 2 * covered < couples:
            moves = [(2 * p + 1, 2 * (p + covered) + 1) for p in range(couples - covered)]
            window = merged(sent_narrow(window, axis, both_ways(count, moves)), window)
            covered *= 2
        moves = [(2 * p + 1, 2 * p + 3) for p in range(couples - 1)]
        nearer = sent_narrow(window, axis, both_ways(count, moves))
        if 1 + covered < couples:
            moves = [(2 * p + 1, 2 * (p + 1 + covered) + 1) for p in range(couples - 1 - covered)]
            nearer = merged(sent_narrow(window, axis, both_ways(count, moves)), nearer)
        incoming = unpacked(nearer)[0]
    other = lax.ppermute(incoming, axis, swap)
    own = lower_rate[:, None, None] * incoming + lower
    return jnp.where(odd, own, other), jnp.where(odd, other, own), held


def passed_along(value, axis, steps):
    count = lax.axis_size(axis)
    pairs = [(source, (source + steps) % count) for source in range(count)]
    return lax.ppermute(value, axis, pairs)


def decay_logs(exponent, boundary, length):
    count, heads = exponent.shape
    rate = jnp.log(1.0 - exponent.astype(jnp.float32) / 65536.0)
    spread = jnp.broadcast_to(rate[:, None, :], (count, length, heads))
    opening = (jnp.arange(length) == 0)[None, :, None] & (boundary == 1)[:, None, None]
    return spread + jnp.where(opening, math.log(0.5), 0.0).astype(spread.dtype)


def projections(inputs, gain, heads):
    rows = inputs.shape[0]
    widened = inputs.astype(jnp.float32)
    result = []
    for index in range(3):
        rounded = lax.optimization_barrier((widened * gain[index]).astype(jnp.bfloat16))
        result.append(rounded.reshape(rows, heads, -1))
    return result


def local(inputs, out_grad, gains, exponent, boundary):
    block = inputs[0]
    grad_block = out_grad[0]
    gain = gains[0]
    rows, width = block.shape
    heads = exponent.shape[2]
    head_dim = width // heads
    scale = 1.0 / head_dim
    query_half, key_half, value_half = projections(block, gain, heads)
    grad_half = grad_block.reshape(rows, heads, head_dim)
    queries = query_half.astype(jnp.float32)
    key_rows = key_half.astype(jnp.float32)
    value_rows = value_half.astype(jnp.float32)
    grad_rows = grad_half.astype(jnp.float32)
    logs = decay_logs(exponent[0], boundary[0], CH).reshape(rows, heads)
    cumul = jnp.cumsum(logs, axis=0)
    growth = jnp.exp(cumul)
    tail = jnp.exp(cumul[-1][None, :] - cumul)
    forward_part = jnp.einsum(
        "shd,she->hde", key_rows * tail[:, :, None], value_rows, precision=HIGH
    )
    adjoint_part = scale * jnp.einsum(
        "shd,she->hde", queries * growth[:, :, None], grad_rows, precision=HIGH
    )
    whole_decay = jnp.exp(cumul[-1])
    cum_heads = cumul.T
    gap = cum_heads[:, :, None] - cum_heads[:, None, :]
    lower = jnp.arange(rows)[:, None] >= jnp.arange(rows)[None, :]
    decay = jnp.where(lower[None], jnp.exp(jnp.minimum(gap, 0.0)), 0.0)
    mixing = (
        jnp.einsum("thd,shd->hts", grad_half, value_half, preferred_element_type=jnp.float32)
        * decay
    )
    query_near = scale * jnp.einsum("hts,shd->thd", mixing, key_rows, precision=HIGH)
    key_near = scale * jnp.einsum("hts,thd->shd", mixing, queries, precision=HIGH)
    attention = (
        jnp.einsum("thd,shd->hts", query_half, key_half, preferred_element_type=jnp.float32) * decay
    )
    value_near = scale * jnp.einsum("hts,the->she", attention, grad_rows, precision=HIGH)
    near_total = grad_block.astype(jnp.float32)
    near_total = near_total + gain[0] * query_near.reshape(rows, width)
    near_total = near_total + gain[1] * key_near.reshape(rows, width)
    near_total = near_total + gain[2] * value_near.reshape(rows, width)
    near_round = near_total.astype(jnp.bfloat16)
    near_received = near_round
    state_in, adjoint_in, near_received = scans_in(
        forward_part, adjoint_part, whole_decay, "ctx", near_received
    )
    query_far = (
        scale * growth[:, :, None] * jnp.einsum("the,hde->thd", grad_rows, state_in, precision=HIGH)
    )
    key_far = tail[:, :, None] * jnp.einsum("she,hde->shd", value_rows, adjoint_in, precision=HIGH)
    value_far = tail[:, :, None] * jnp.einsum("shd,hde->she", key_rows, adjoint_in, precision=HIGH)
    far_total = gain[0] * query_far.reshape(rows, width)
    far_total = far_total + gain[1] * key_far.reshape(rows, width)
    far_total = far_total + gain[2] * value_far.reshape(rows, width)
    far_round = far_total.astype(jnp.bfloat16)
    near_kept, far_kept = lax.optimization_barrier((near_received, far_round))
    outgoing = (near_kept.astype(jnp.float32) + far_kept.astype(jnp.float32)).astype(jnp.bfloat16)
    received = passed_along(outgoing, "section", -1)
    return received[None]


def solution(mesh):
    in_specs = (
        P("section", "ctx", None),
        P("section", "ctx", None),
        P("section", None, None),
        P("section", "ctx", None),
        P("section", "ctx"),
    )
    out_specs = P("section", "ctx", None)
    return jax.shard_map(local, mesh=mesh, in_specs=in_specs, out_specs=out_specs, check_vma=False)
```

```python
import math

import jax
import jax.numpy as jnp
from jax import lax
from jax.sharding import PartitionSpec as P

CH = 64


HIGH = lax.Precision.HIGH


def packed(state, rate):
    tile = jnp.broadcast_to(rate[:, None, None], (state.shape[0], 8, state.shape[2]))
    return jnp.concatenate([state, tile], axis=1)


def unpacked(message):
    width = message.shape[1] - 8
    return message[:, :width], message[:, width, 0]


def narrow(message):
    state, rate = unpacked(message)
    high = rate.astype(jnp.bfloat16)
    low = (rate - high.astype(jnp.float32)).astype(jnp.bfloat16)
    rows = jnp.stack([high, low] + [jnp.zeros_like(high)] * 6, axis=1)
    tile = jnp.broadcast_to(rows[:, :, None], (state.shape[0], 8, state.shape[2]))
    return jnp.concatenate([state.astype(jnp.bfloat16), tile], axis=1)


def widen(message):
    width = message.shape[1] - 8
    rate = message[:, width, 0].astype(jnp.float32) + message[:, width + 1, 0].astype(jnp.float32)
    return packed(message[:, :width].astype(jnp.float32), rate)


def sent_narrow(message, axis, pairs):
    return widen(lax.ppermute(narrow(message), axis, pairs))


def merged(farther, nearer):
    far_state, far_rate = unpacked(farther)
    near_state, near_rate = unpacked(nearer)
    return packed(near_rate[:, None, None] * far_state + near_state, far_rate * near_rate)


def both_ways(count, moves):
    return list(moves) + [(count - 1 - source, count - 1 - target) for source, target in moves]


def scans_in(forward_part, backward_part, rate, axis, held):
    count = lax.axis_size(axis)
    if count == 1:
        return jnp.zeros_like(forward_part), jnp.zeros_like(backward_part), held
    assert count % 2 == 0
    odd = lax.axis_index(axis) % 2 == 1
    couples = count // 2
    swap = [(2 * p, 2 * p + 1) for p in range(couples)] + [(2 * p + 1, 2 * p) for p in range(couples)]
    mine = jnp.where(odd, forward_part, backward_part)
    sent = packed(jnp.where(odd, backward_part, forward_part), rate)
    message = lax.ppermute(sent, axis, swap)
    lower, lower_rate = unpacked(message)
    window = rate[:, None, None] * message + packed(mine, jnp.zeros_like(rate))
    if couples <= 4:
        incoming = jnp.zeros_like(mine)
        weight = jnp.ones_like(rate)
        for step in range(1, couples):
            moves = [(2 * p + 1, 2 * (p + step) + 1) for p in range(couples - step)]
            if step == couples - 1:
                bare = unpacked(window)[0].astype(jnp.bfloat16)
                got = lax.ppermute(bare, axis, both_ways(count, moves)).astype(jnp.float32)
                incoming = incoming + weight[:, None, None] * got
                continue
            got, got_rate = unpacked(sent_narrow(window, axis, both_ways(count, moves)))
            incoming = incoming + weight[:, None, None] * got
            weight = weight * got_rate
    else:
        covered = 1
        while 2 * covered < couples:
            moves = [(2 * p + 1, 2 * (p + covered) + 1) for p in range(couples - covered)]
            window = merged(sent_narrow(window, axis, both_ways(count, moves)), window)
            covered *= 2
        moves = [(2 * p + 1, 2 * p + 3) for p in range(couples - 1)]
        nearer = sent_narrow(window, axis, both_ways(count, moves))
        if 1 + covered < couples:
            moves = [(2 * p + 1, 2 * (p + 1 + covered) + 1) for p in range(couples - 1 - covered)]
            nearer = merged(sent_narrow(window, axis, both_ways(count, moves)), nearer)
        incoming = unpacked(nearer)[0]
    incoming, held = lax.optimization_barrier((incoming, held))
    other = lax.ppermute(incoming, axis, swap)
    own = lower_rate[:, None, None] * incoming + lower
    return jnp.where(odd, own, other), jnp.where(odd, other, own), held


def passed_along(value, axis, steps):
    count = lax.axis_size(axis)
    pairs = [(source, (source + steps) % count) for source in range(count)]
    return lax.ppermute(value, axis, pairs)


def decay_logs(exponent, boundary, length):
    count, heads = exponent.shape
    rate = jnp.log(1.0 - exponent.astype(jnp.float32) / 65536.0)
    spread = jnp.broadcast_to(rate[:, None, :], (count, length, heads))
    opening = (jnp.arange(length) == 0)[None, :, None] & (boundary == 1)[:, None, None]
    return spread + jnp.where(opening, math.log(0.5), 0.0).astype(spread.dtype)


def projections(inputs, gain, heads):
    rows = inputs.shape[0]
    widened = inputs.astype(jnp.float32)
    result = []
    for index in range(3):
        rounded = lax.optimization_barrier((widened * gain[index]).astype(jnp.bfloat16))
        result.append(rounded.reshape(rows, heads, -1))
    return result


def local(inputs, out_grad, gains, exponent, boundary):
    block = inputs[0]
    grad_block = out_grad[0]
    gain = gains[0]
    rows, width = block.shape
    heads = exponent.shape[2]
    head_dim = width // heads
    scale = 1.0 / head_dim
    query_half, key_half, value_half = projections(block, gain, heads)
    grad_half = grad_block.reshape(rows, heads, head_dim)
    queries = query_half.astype(jnp.float32)
    key_rows = key_half.astype(jnp.float32)
    value_rows = value_half.astype(jnp.float32)
    grad_rows = grad_half.astype(jnp.float32)
    logs = decay_logs(exponent[0], boundary[0], CH).reshape(rows, heads)
    cumul = jnp.cumsum(logs, axis=0)
    growth = jnp.exp(cumul)
    tail = jnp.exp(cumul[-1][None, :] - cumul)
    forward_part = jnp.einsum(
        "shd,she->hde", key_rows * tail[:, :, None], value_rows, precision=HIGH
    )
    adjoint_part = scale * jnp.einsum(
        "shd,she->hde", queries * growth[:, :, None], grad_rows, precision=HIGH
    )
    whole_decay = jnp.exp(cumul[-1])
    cum_heads = cumul.T
    gap = cum_heads[:, :, None] - cum_heads[:, None, :]
    lower = jnp.arange(rows)[:, None] >= jnp.arange(rows)[None, :]
    decay = jnp.where(lower[None], jnp.exp(jnp.minimum(gap, 0.0)), 0.0)
    mixing = (
        jnp.einsum("thd,shd->hts", grad_half, value_half, preferred_element_type=jnp.float32)
        * decay
    )
    query_near = scale * jnp.einsum("hts,shd->thd", mixing, key_rows, precision=HIGH)
    key_near = scale * jnp.einsum("hts,thd->shd", mixing, queries, precision=HIGH)
    attention = (
        jnp.einsum("thd,shd->hts", query_half, key_half, preferred_element_type=jnp.float32) * decay
    )
    value_near = scale * jnp.einsum("hts,the->she", attention, grad_rows, precision=HIGH)
    near_total = grad_block.astype(jnp.float32)
    near_total = near_total + gain[0] * query_near.reshape(rows, width)
    near_total = near_total + gain[1] * key_near.reshape(rows, width)
    near_total = near_total + gain[2] * value_near.reshape(rows, width)
    near_round = near_total.astype(jnp.bfloat16)
    near_received = near_round
    state_in, adjoint_in, near_received = scans_in(
        forward_part, adjoint_part, whole_decay, "ctx", near_received
    )
    query_far = (
        scale * growth[:, :, None] * jnp.einsum("the,hde->thd", grad_rows, state_in, precision=HIGH)
    )
    key_far = tail[:, :, None] * jnp.einsum("she,hde->shd", value_rows, adjoint_in, precision=HIGH)
    value_far = tail[:, :, None] * jnp.einsum("shd,hde->she", key_rows, adjoint_in, precision=HIGH)
    far_total = gain[0] * query_far.reshape(rows, width)
    far_total = far_total + gain[1] * key_far.reshape(rows, width)
    far_total = far_total + gain[2] * value_far.reshape(rows, width)
    far_round = far_total.astype(jnp.bfloat16)
    near_kept, far_kept = lax.optimization_barrier((near_received, far_round))
    outgoing = (near_kept.astype(jnp.float32) + far_kept.astype(jnp.float32)).astype(jnp.bfloat16)
    received = passed_along(outgoing, "section", -1)
    return received[None]


def solution(mesh):
    in_specs = (
        P("section", "ctx", None),
        P("section", "ctx", None),
        P("section", None, None),
        P("section", "ctx", None),
        P("section", "ctx"),
    )
    out_specs = P("section", "ctx", None)
    return jax.shard_map(local, mesh=mesh, in_specs=in_specs, out_specs=out_specs, check_vma=False)
```
